512 devices in a mesh: seg: 32 (over x_lo, z, core), tpl: 16 (over x_hi, y).
Axes of the slice: x: 4 (x_hi: 2, x_lo: 2; x = x_hi * 2 + x_lo), y: 8, z: 8, core: 2. Of those that a mesh axis runs over, the one named last changes fastest.
Arguments:
- strain: bfloat16 [1024, 2, 2, 128, 128], P(('seg', 'tpl')), may hold values from -6 to 6
- templates: bfloat16 [64, 2, 128, 128], P('tpl'), may hold values from -6 to 6
- psd: float32 [2, 128, 128], P(None, 'seg'), may hold values from 0.25 to 4
- flags: int32 [1024], P(('seg', 'tpl')), may hold values 0 or 1
- assign: int32 [64], replicated, may hold values from 0 to 7
Outputs:
- peak: float32 [1024, 64], P(('seg', 'tpl'))
- best: float32 [1024, 8], P(('seg', 'tpl'))
The draws below stay inside these ranges and needn't reach their ends.
All inputs are finite; a program needn't handle non-finite values. No bound on the sum of `flags` on one device may be relied on, other than what follows from the above.
Results may differ from the reference program's by a relative error of at most 0.0015.
Values may be sent and summed in bfloat16 or wider, within the bound.
No kernel may reach another device: no remote copies, remote signals or barrier semaphores. Data moves between devices by JAX's collectives and lax.ppermute only.
A program may use at most 64 MiB of HBM per device.

```python
import math
import jax
import jax.numpy as jnp
from jax import lax

N1 = 128
N2 = 128
BINS = 16384
BLOCKS = 8
SEGMENTS = 1024
TEMPLATES = 64


def place_ends(drawn, own_key, low, top_value):
    longest = drawn.shape.index(max(drawn.shape))
    spots = []
    for shift in (0, 1):
        where = [jax.random.randint(jax.random.fold_in(own_key, axis), (), 0, length) for axis, length in enumerate(drawn.shape)]
        where[longest] = (where[longest] + shift) % drawn.shape[longest]
        spots.append(tuple(where))
    return drawn.at[spots[0]].set(low).at[spots[1]].set(top_value)


def levels(stream_key, extent, cuts, smallest, largest):
    factor_of = 1.0
    for dim, parts in cuts:
        heights = jax.random.uniform(jax.random.fold_in(jax.random.fold_in(stream_key, 6), dim), (parts,), jnp.float32, smallest / len(cuts), largest / len(cuts))
        factor_of = factor_of * jnp.repeat(jnp.exp(heights), extent[dim] // parts).reshape((-1,) + (1,) * (len(extent) - 1 - dim))
    return factor_of


def bell_draw(own_key, dims, deviation, limit, shards=(), held_as=jnp.bfloat16):
    entries = jax.random.normal(own_key, dims, jnp.float32) * deviation
    if len(shards) > 0:
        entries = levels(own_key, dims, shards, -0.22, 0.18) * entries
    return jnp.clip(entries, min=-limit, max=limit).astype(held_as)


def setup_inputs(seed: int = 0) -> dict:
    seeds = jax.random.split(jax.random.key(seed), 6)
    strain = bell_draw(seeds[0], (SEGMENTS, 2, 2, N1, N2), 1.0, 6.0, ((0, 512),))
    templates = bell_draw(seeds[1], (TEMPLATES, 2, N1, N2), 1.0, 6.0, ((0, 16),))
    psd = jnp.clip(jnp.exp(math.log(4.0) - 2.7725887 * jax.random.uniform(seeds[2], (2, N1, N2), jnp.float32) ** levels(seeds[2], (2, N1, N2), ((1, 32),), -0.2, 0.2)), 0.25, 4.0)
    flags = place_ends((jax.random.randint(seeds[3], (SEGMENTS,), 0, 4) < 3).astype(jnp.int32), jax.random.fold_in(seeds[3], 1), 0, 1)
    assign = place_ends(jax.random.randint(seeds[4], (TEMPLATES,), 0, BLOCKS), jax.random.fold_in(seeds[4], 1), 0, BLOCKS - 1).astype(jnp.int32)
    return dict(strain=strain, templates=templates, psd=psd, flags=flags, assign=assign)


def make_tables():
    row_idx = jnp.arange(N1, dtype=jnp.int32)
    col_idx = jnp.arange(N2, dtype=jnp.int32)
    ang_one = 2.0 * math.pi * (row_idx[:, None] * row_idx[None, :] % N1).astype(jnp.float32) / N1
    cos_one, sin_one = (jnp.cos(ang_one), jnp.sin(ang_one))
    first = jnp.concatenate([jnp.concatenate([cos_one, -sin_one], 1), jnp.concatenate([sin_one, cos_one], 1)], 0).astype(jnp.bfloat16)
    ang_two = 2.0 * math.pi * (col_idx[:, None] * col_idx[None, :] % N2).astype(jnp.float32) / N2
    cos_two, sin_two = (jnp.cos(ang_two), jnp.sin(ang_two))
    second = jnp.concatenate([jnp.concatenate([cos_two, sin_two], 1), jnp.concatenate([-sin_two, cos_two], 1)], 0).astype(jnp.bfloat16)
    ang_tw = 2.0 * math.pi * (row_idx[:, None] * col_idx[None, :] % BINS).astype(jnp.float32) / BINS
    return (first, second, jnp.cos(ang_tw), jnp.sin(ang_tw))

def power_peak(seg_data, tmpl, weights, tables):
    first, second, tw_cos, tw_sin = tables
    count = seg_data.shape[0]
    h_re = tmpl[0].astype(jnp.float32)
    h_im = tmpl[1].astype(jnp.float32)
    d_re = seg_data[:, :, 0].astype(jnp.float32)
    d_im = seg_data[:, :, 1].astype(jnp.float32)
    q_re = (d_re * h_re + d_im * h_im) * weights
    q_im = (d_im * h_re - d_re * h_im) * weights
    stacked = jnp.stack([q_re, q_im], 2).reshape(count * 2, 2 * N1, N2).astype(jnp.bfloat16)
    rotated = jnp.einsum('ij,bjk->bik', first.astype(jnp.float32), stacked.astype(jnp.float32))
    y_re, y_im = (rotated[:, :N1], rotated[:, N1:])
    z_re = y_re * tw_cos - y_im * tw_sin
    z_im = y_re * tw_sin + y_im * tw_cos
    twisted = jnp.concatenate([z_re, z_im], -1).astype(jnp.bfloat16)
    series = jnp.einsum('bik,kl->bil', twisted.astype(jnp.float32), second.astype(jnp.float32))
    power = series[:, :, :N2] ** 2 + series[:, :, N2:] ** 2
    power = power.reshape(count, 2, N1, N2)
    sigma2 = lax.optimization_barrier(jnp.sum((h_re * h_re + h_im * h_im) * weights, axis=(1, 2)))
    rho2 = lax.optimization_barrier(jnp.sum(power / sigma2[None, :, None, None], axis=1))
    return lax.optimization_barrier(jnp.max(rho2, axis=(1, 2)))

def reference(strain, templates, psd, flags, assign):
    weights = 1.0 / psd
    tables = make_tables()

    def one_segment(seg_data):

        def one_template(tmpl):
            return power_peak(seg_data[None], tmpl, weights, tables)[0]
        return lax.map(one_template, templates)
    rho2 = lax.map(one_segment, strain)
    peak = jnp.sqrt(rho2) * flags.astype(jnp.float32)[:, None]
    onehot = assign[:, None] == jnp.arange(BLOCKS, dtype=jnp.int32)[None, :]
    best = lax.optimization_barrier(jnp.max(jnp.where(onehot[None], peak[:, :, None], jnp.float32(0.0)), axis=1))
    return (peak, best)
```

```python
import functools
import math

import jax
import jax.numpy as jnp
from jax import lax
from jax.experimental import pallas as pl
from jax.experimental.pallas import tpu as pltpu
from jax.sharding import Mesh
from jax.sharding import PartitionSpec as P

N1 = 128
N2 = 128
BINS = 16384
BLOCKS = 8
TB = 4


def make_tables():
    row_idx = jnp.arange(N1, dtype=jnp.int32)
    col_idx = jnp.arange(N2, dtype=jnp.int32)
    ang_one = 2.0 * math.pi * (row_idx[:, None] * row_idx[None, :] % N1).astype(jnp.float32) / N1
    cos_one, sin_one = (jnp.cos(ang_one), jnp.sin(ang_one))
    first = jnp.concatenate(
        [jnp.concatenate([cos_one, -sin_one], 1), jnp.concatenate([sin_one, cos_one], 1)], 0
    ).astype(jnp.bfloat16)
    ang_two = 2.0 * math.pi * (col_idx[:, None] * col_idx[None, :] % N2).astype(jnp.float32) / N2
    cos_two, sin_two = (jnp.cos(ang_two), jnp.sin(ang_two))
    second = jnp.concatenate(
        [jnp.concatenate([cos_two, sin_two], 1), jnp.concatenate([-sin_two, cos_two], 1)], 0
    ).astype(jnp.bfloat16)
    ang_tw = 2.0 * math.pi * (row_idx[:, None] * col_idx[None, :] % BINS).astype(jnp.float32) / BINS
    return (first, second, jnp.cos(ang_tw), jnp.sin(ang_tw))


def template_norm(tmpl, weights):
    h_re = tmpl[0].astype(jnp.float32)
    h_im = tmpl[1].astype(jnp.float32)
    return jnp.sum((h_re * h_re + h_im * h_im) * weights, axis=(1, 2))


def search_kernel(n_tb, sidx_ref, isig_ref, strain_ref, tmpl_ref, w_ref, m1_ref, m2_ref,
                  tc_ref, ts_ref, out_ref, q_ref, y_ref, z_ref):
    nb = 2 * TB

    def step(i, carry):
        s = i // n_tb
        tb = i % n_tb
        seg = sidx_ref[s]
        for k in range(TB):
            t = tb * TB + k
            h_re = tmpl_ref[t, 0].astype(jnp.float32)
            h_im = tmpl_ref[t, 1].astype(jnp.float32)
            for d in range(2):
                d_re = strain_ref[seg, d, 0].astype(jnp.float32)
                d_im = strain_ref[seg, d, 1].astype(jnp.float32)
                w = w_ref[d]
                q_re = (d_re * h_re + d_im * h_im) * w
                q_im = (d_im * h_re - d_re * h_im) * w
                col = (2 * k + d) * N2
                q_ref[0:N1, col:col + N2] = q_re.astype(jnp.bfloat16)
                q_ref[N1:2 * N1, col:col + N2] = q_im.astype(jnp.bfloat16)
        y_ref[...] = jnp.dot(m1_ref[...], q_ref[...], preferred_element_type=jnp.float32)
        tc = tc_ref[...]
        ts = ts_ref[...]
        for b in range(nb):
            col = b * N2
            y_re = y_ref[0:N1, col:col + N2]
            y_im = y_ref[N1:2 * N1, col:col + N2]
            z_re = y_re * tc - y_im * ts
            z_im = y_re * ts + y_im * tc
            z_ref[col:col + N2, 0:N2] = z_re.astype(jnp.bfloat16)
            z_ref[col:col + N2, N2:2 * N2] = z_im.astype(jnp.bfloat16)
        x = jnp.dot(z_ref[...], m2_ref[...], preferred_element_type=jnp.float32)
        for k in range(TB):
            t = tb * TB + k
            acc = None
            for d in range(2):
                r0 = (2 * k + d) * N1
                x_re = x[r0:r0 + N1, 0:N2]
                x_im = x[r0:r0 + N1, N2:2 * N2]
                p = (x_re * x_re + x_im * x_im) * isig_ref[2 * t + d]
                acc = p if acc is None else acc + p
            out_ref[s, pl.ds(t, 1), :] = jnp.max(acc, axis=0, keepdims=True)
        return carry

    lax.fori_loop(0, sidx_ref.shape[0] * n_tb, step, 0)


def run_search(sidx, isig, strain, tmpl, weights, tables):
    m1, m2, tc, ts = tables
    n_s = sidx.shape[0]
    n_t = tmpl.shape[0]
    n_tb = n_t // TB
    vmem = pltpu.VMEM
    smem = pltpu.SMEM
    ffts = n_s * n_t * 2
    cost = pl.CostEstimate(
        flops=ffts * 2 * (2 * 256 * 256 * 128),
        transcendentals=0,
        bytes_accessed=strain.size * 2 + tmpl.size * 2 + weights.size * 4,
    )
    out = pl.pallas_call(
        functools.partial(search_kernel, n_tb),
        out_shape=jax.ShapeDtypeStruct((n_s, n_t, N2), jnp.float32),
        in_specs=[pl.BlockSpec(memory_space=smem), pl.BlockSpec(memory_space=smem)]
        + [pl.BlockSpec(memory_space=vmem)] * 7,
        out_specs=pl.BlockSpec(memory_space=vmem),
        scratch_shapes=[
            pltpu.VMEM((2 * N1, 2 * TB * N2), jnp.bfloat16),
            pltpu.VMEM((2 * N1, 2 * TB * N2), jnp.float32),
            pltpu.VMEM((2 * TB * N1, 2 * N2), jnp.bfloat16),
        ],
        cost_estimate=cost,
    )(sidx, isig, strain, tmpl, weights, m1, m2, tc, ts)
    return jnp.max(out, axis=-1)


def body(strain, templates, psd, flags, assign):
    ya = lax.axis_index("ya")
    n_ya = lax.axis_size("ya")
    rows_here = psd.shape[1]
    psd_t = jnp.transpose(psd, (1, 0, 2)).reshape(rows_here, -1)
    gathered = lax.all_gather(psd_t, "seg", axis=0, tiled=True)
    full_psd = jnp.transpose(gathered.reshape(-1, 2, N2), (1, 0, 2))
    weights = 1.0 / full_psd
    tables = make_tables()
    tmpl_all = lax.all_gather(templates, ("xh", "yb"), axis=0, tiled=True)
    piece = lax.all_gather(strain, "ya", axis=0, tiled=True)
    sigma2 = jax.vmap(lambda tmpl: template_norm(tmpl, weights))(tmpl_all)
    isig = (1.0 / sigma2).reshape(-1)

    own_count = strain.shape[0]
    own_idx = jnp.arange(own_count, dtype=jnp.int32)
    own_rows = run_search(own_idx, isig, strain, tmpl_all, weights, tables)

    own_rows, piece = lax.optimization_barrier((own_rows, piece))
    shifts = jnp.arange(1, n_ya, dtype=jnp.int32)
    other_blocks = (ya + shifts) % n_ya
    other_idx = (other_blocks[:, None] * own_count + own_idx[None, :]).reshape(-1)
    other_rows = run_search(other_idx, isig, piece, tmpl_all, weights, tables)

    rolled = jnp.concatenate([own_rows, other_rows], 0).reshape(n_ya, own_count, -1)
    grouped = jnp.roll(rolled, ya, axis=0)
    got = lax.all_to_all(grouped, "ya", split_axis=0, concat_axis=0, tiled=True)
    n_xh = lax.axis_size("xh")
    n_yb = lax.axis_size("yb")
    got = got.reshape(n_ya, own_count, n_xh, n_yb, -1)
    rho2 = jnp.transpose(got, (1, 2, 0, 3, 4)).reshape(own_count, -1)

    peak = jnp.sqrt(rho2) * flags.astype(jnp.float32)[:, None]
    onehot = assign[:, None] == jnp.arange(BLOCKS, dtype=jnp.int32)[None, :]
    best = jnp.max(jnp.where(onehot[None], peak[:, :, None], jnp.float32(0.0)), axis=1)
    return (peak, best)


def solution(mesh):
    n_seg, n_tpl = mesh.devices.shape
    n_y = 8
    n_xh = n_tpl // n_y
    sub = Mesh(
        mesh.devices.reshape(n_seg, n_xh, n_y // 2, 2),
        ("seg", "xh", "ya", "yb"),
    )
    rows = ("seg", "xh", "ya", "yb")
    placed = (
        P(rows, None, None, None, None),
        P(("xh", "ya", "yb"), None, None, None),
        P(None, "seg", None),
        P(rows),
        P(),
    )
    return jax.shard_map(
        body,
        mesh=sub,
        in_specs=placed,
        out_specs=(P(rows, None), P(rows, None)),
        check_vma=False,
    )
```

```python
import functools
import math

import jax
import jax.numpy as jnp
from jax import lax
from jax.experimental import pallas as pl
from jax.experimental.pallas import tpu as pltpu
from jax.sharding import Mesh
from jax.sharding import PartitionSpec as P

N1 = 128
N2 = 128
BINS = 16384
BLOCKS = 8
TB = 4


def make_tables():
    row_idx = jnp.arange(N1, dtype=jnp.int32)
    col_idx = jnp.arange(N2, dtype=jnp.int32)
    ang_one = 2.0 * math.pi * (row_idx[:, None] * row_idx[None, :] % N1).astype(jnp.float32) / N1
    cos_one, sin_one = (jnp.cos(ang_one), jnp.sin(ang_one))
    first = jnp.concatenate(
        [jnp.concatenate([cos_one, -sin_one], 1), jnp.concatenate([sin_one, cos_one], 1)], 0
    ).astype(jnp.bfloat16)
    ang_two = 2.0 * math.pi * (col_idx[:, None] * col_idx[None, :] % N2).astype(jnp.float32) / N2
    cos_two, sin_two = (jnp.cos(ang_two), jnp.sin(ang_two))
    second = jnp.concatenate(
        [jnp.concatenate([cos_two, sin_two], 1), jnp.concatenate([-sin_two, cos_two], 1)], 0
    ).astype(jnp.bfloat16)
    ang_tw = 2.0 * math.pi * (row_idx[:, None] * col_idx[None, :] % BINS).astype(jnp.float32) / BINS
    return (first, second, jnp.cos(ang_tw), jnp.sin(ang_tw))


def template_norm(tmpl, weights):
    h_re = tmpl[0].astype(jnp.float32)
    h_im = tmpl[1].astype(jnp.float32)
    return jnp.sum((h_re * h_re + h_im * h_im) * weights, axis=(1, 2))


def search_kernel(n_tb, sidx_ref, isig_ref, strain_ref, tmpl_ref, w_ref, m1_ref, m2_ref,
                  tc_ref, ts_ref, out_ref, q_ref, y_ref, z_ref):
    nb = 2 * TB

    def step(i, carry):
        s = i // n_tb
        tb = i % n_tb
        seg = sidx_ref[s]
        for k in range(TB):
            t = tb * TB + k
            h_re = tmpl_ref[t, 0].astype(jnp.float32)
            h_im = tmpl_ref[t, 1].astype(jnp.float32)
            for d in range(2):
                d_re = strain_ref[seg, d, 0].astype(jnp.float32)
                d_im = strain_ref[seg, d, 1].astype(jnp.float32)
                w = w_ref[d]
                q_re = (d_re * h_re + d_im * h_im) * w
                q_im = (d_im * h_re - d_re * h_im) * w
                col = (2 * k + d) * N2
                q_ref[0:N1, col:col + N2] = q_re.astype(jnp.bfloat16)
                q_ref[N1:2 * N1, col:col + N2] = q_im.astype(jnp.bfloat16)
        y_ref[...] = jnp.dot(m1_ref[...], q_ref[...], preferred_element_type=jnp.float32)
        tc = tc_ref[...]
        ts = ts_ref[...]
        for b in range(nb):
            col = b * N2
            y_re = y_ref[0:N1, col:col + N2]
            y_im = y_ref[N1:2 * N1, col:col + N2]
            z_re = y_re * tc - y_im * ts
            z_im = y_re * ts + y_im * tc
            z_ref[col:col + N2, 0:N2] = z_re.astype(jnp.bfloat16)
            z_ref[col:col + N2, N2:2 * N2] = z_im.astype(jnp.bfloat16)
        x = jnp.dot(z_ref[...], m2_ref[...], preferred_element_type=jnp.float32)
        for k in range(TB):
            t = tb * TB + k
            acc = None
            for d in range(2):
                r0 = (2 * k + d) * N1
                x_re = x[r0:r0 + N1, 0:N2]
                x_im = x[r0:r0 + N1, N2:2 * N2]
                p = (x_re * x_re + x_im * x_im) * isig_ref[2 * t + d]
                acc = p if acc is None else acc + p
            out_ref[s, pl.ds(t, 1), :] = jnp.max(acc, axis=0, keepdims=True)
        return carry

    lax.fori_loop(0, sidx_ref.shape[0] * n_tb, step, 0)


def run_search(sidx, isig, strain, tmpl, weights, tables):
    m1, m2, tc, ts = tables
    n_s = sidx.shape[0]
    n_t = tmpl.shape[0]
    n_tb = n_t // TB
    vmem = pltpu.VMEM
    smem = pltpu.SMEM
    ffts = n_s * n_t * 2
    cost = pl.CostEstimate(
        flops=ffts * 2 * (2 * 256 * 256 * 128),
        transcendentals=0,
        bytes_accessed=strain.size * 2 + tmpl.size * 2 + weights.size * 4,
    )
    out = pl.pallas_call(
        functools.partial(search_kernel, n_tb),
        out_shape=jax.ShapeDtypeStruct((n_s, n_t, N2), jnp.float32),
        in_specs=[pl.BlockSpec(memory_space=smem), pl.BlockSpec(memory_space=smem)]
        + [pl.BlockSpec(memory_space=vmem)] * 7,
        out_specs=pl.BlockSpec(memory_space=vmem),
        scratch_shapes=[
            pltpu.VMEM((2 * N1, 2 * TB * N2), jnp.bfloat16),
            pltpu.VMEM((2 * N1, 2 * TB * N2), jnp.float32),
            pltpu.VMEM((2 * TB * N1, 2 * N2), jnp.bfloat16),
        ],
        cost_estimate=cost,
    )(sidx, isig, strain, tmpl, weights, m1, m2, tc, ts)
    return jnp.max(out, axis=-1)


def shifted(x, axes, size, k):
    return lax.ppermute(x, axes, [(i, (i + k) % size) for i in range(size)])


def body(strain, templates, psd, flags, assign):
    ya = lax.axis_index("ya")
    n_ya = lax.axis_size("ya")
    n_xh = lax.axis_size("xh")
    n_yb = lax.axis_size("yb")
    n_g = n_xh * n_yb
    g = lax.axis_index("xh") * n_yb + lax.axis_index("yb")

    rows_here = psd.shape[1]
    gathered = jnp.transpose(psd, (1, 0, 2)).reshape(rows_here, -1)
    for axis in ("sc", "sz", "sx"):
        gathered = lax.all_gather(gathered, axis, axis=0, tiled=True)
    full_psd = jnp.transpose(gathered.reshape(-1, 2, N2), (1, 0, 2))
    weights = 1.0 / full_psd
    tables = make_tables()

    tmpl_rel = jnp.concatenate(
        [templates] + [shifted(templates, ("xh", "yb"), n_g, k) for k in range(1, n_g)], 0
    )
    piece = jnp.concatenate([shifted(strain, "ya", n_ya, k) for k in range(1, n_ya)], 0)
    sigma2 = jax.vmap(lambda tmpl: template_norm(tmpl, weights))(tmpl_rel)
    isig = (1.0 / sigma2).reshape(-1)

    own_count = strain.shape[0]
    own_idx = jnp.arange(own_count, dtype=jnp.int32)
    own_rows = run_search(own_idx, isig, strain, tmpl_rel, weights, tables)
    own_rows, piece = lax.optimization_barrier((own_rows, piece))
    other_idx = jnp.arange(piece.shape[0], dtype=jnp.int32)
    other_rows = run_search(other_idx, isig, piece, tmpl_rel, weights, tables)
    other_rows = other_rows.reshape(n_ya - 1, own_count, -1)

    blocks = [own_rows] + [shifted(other_rows[k - 1], "ya", n_ya, -k) for k in range(1, n_ya)]
    blocks = jnp.stack(blocks, 0).reshape(n_ya, own_count, n_g, -1)
    src_k = (jnp.arange(n_ya, dtype=jnp.int32) - ya) % n_ya
    src_t = (g - jnp.arange(n_g, dtype=jnp.int32)) % n_g
    ordered = jnp.take(jnp.take(blocks, src_k, axis=0), src_t, axis=2)
    ordered = ordered.reshape(n_ya, own_count, n_xh, n_yb, -1)
    rho2 = jnp.transpose(ordered, (1, 2, 0, 3, 4)).reshape(own_count, -1)

    peak = jnp.sqrt(rho2) * flags.astype(jnp.float32)[:, None]
    onehot = assign[:, None] == jnp.arange(BLOCKS, dtype=jnp.int32)[None, :]
    best = jnp.max(jnp.where(onehot[None], peak[:, :, None], jnp.float32(0.0)), axis=1)
    return (peak, best)


def solution(mesh):
    n_seg, n_tpl = mesh.devices.shape
    n_y = 8
    n_xh = n_tpl // n_y
    n_sz = 8
    n_sx = n_seg // (n_sz * 2)
    sub = Mesh(
        mesh.devices.reshape(n_sx, n_sz, 2, n_xh, n_y // 2, 2),
        ("sx", "sz", "sc", "xh", "ya", "yb"),
    )
    seg = ("sx", "sz", "sc")
    rows = seg + ("xh", "ya", "yb")
    placed = (
        P(rows, None, None, None, None),
        P(("xh", "ya", "yb"), None, None, None),
        P(None, seg, None),
        P(rows),
        P(),
    )
    return jax.shard_map(
        body,
        mesh=sub,
        in_specs=placed,
        out_specs=(P(rows, None), P(rows, None)),
        check_vma=False,
    )
```

```python
import functools
import math

import jax
import jax.numpy as jnp
from jax import lax
from jax.experimental import pallas as pl
from jax.experimental.pallas import tpu as pltpu
from jax.sharding import Mesh
from jax.sharding import PartitionSpec as P

N1 = 128
N2 = 128
BINS = 16384
BLOCKS = 8
TB = 4


def make_tables():
    row_idx = jnp.arange(N1, dtype=jnp.int32)
    col_idx = jnp.arange(N2, dtype=jnp.int32)
    ang_one = 2.0 * math.pi * (row_idx[:, None] * row_idx[None, :] % N1).astype(jnp.float32) / N1
    cos_one, sin_one = (jnp.cos(ang_one), jnp.sin(ang_one))
    first = jnp.concatenate(
        [jnp.concatenate([cos_one, -sin_one], 1), jnp.concatenate([sin_one, cos_one], 1)], 0
    ).astype(jnp.bfloat16)
    ang_two = 2.0 * math.pi * (col_idx[:, None] * col_idx[None, :] % N2).astype(jnp.float32) / N2
    cos_two, sin_two = (jnp.cos(ang_two), jnp.sin(ang_two))
    second = jnp.concatenate(
        [jnp.concatenate([cos_two, sin_two], 1), jnp.concatenate([-sin_two, cos_two], 1)], 0
    ).astype(jnp.bfloat16)
    ang_tw = 2.0 * math.pi * (row_idx[:, None] * col_idx[None, :] % BINS).astype(jnp.float32) / BINS
    return (first, second, jnp.cos(ang_tw), jnp.sin(ang_tw))


def template_norm(tmpl, weights):
    h_re = tmpl[0].astype(jnp.float32)
    h_im = tmpl[1].astype(jnp.float32)
    return jnp.sum((h_re * h_re + h_im * h_im) * weights, axis=(1, 2))


def search_kernel(n_tb, sidx_ref, isig_ref, strain_ref, tmpl_ref, w_ref, m1_ref, m2_ref,
                  tc_ref, ts_ref, out_ref, q_ref, y_ref, z_ref):
    nb = 2 * TB

    def step(i, carry):
        s = i // n_tb
        tb = i % n_tb
        seg = sidx_ref[s]
        for k in range(TB):
            t = tb * TB + k
            h_re = tmpl_ref[t, 0].astype(jnp.float32)
            h_im = tmpl_ref[t, 1].astype(jnp.float32)
            for d in range(2):
                d_re = strain_ref[seg, d, 0].astype(jnp.float32)
                d_im = strain_ref[seg, d, 1].astype(jnp.float32)
                w = w_ref[d]
                q_re = (d_re * h_re + d_im * h_im) * w
                q_im = (d_im * h_re - d_re * h_im) * w
                col = (2 * k + d) * N2
                q_ref[0:N1, col:col + N2] = q_re.astype(jnp.bfloat16)
                q_ref[N1:2 * N1, col:col + N2] = q_im.astype(jnp.bfloat16)
        y_ref[...] = jnp.dot(m1_ref[...], q_ref[...], preferred_element_type=jnp.float32)
        tc = tc_ref[...]
        ts = ts_ref[...]
        for b in range(nb):
            col = b * N2
            y_re = y_ref[0:N1, col:col + N2]
            y_im = y_ref[N1:2 * N1, col:col + N2]
            z_re = y_re * tc - y_im * ts
            z_im = y_re * ts + y_im * tc
            z_ref[col:col + N2, 0:N2] = z_re.astype(jnp.bfloat16)
            z_ref[col:col + N2, N2:2 * N2] = z_im.astype(jnp.bfloat16)
        x = jnp.dot(z_ref[...], m2_ref[...], preferred_element_type=jnp.float32)
        for k in range(TB):
            t = tb * TB + k
            acc = None
            for d in range(2):
                r0 = (2 * k + d) * N1
                x_re = x[r0:r0 + N1, 0:N2]
                x_im = x[r0:r0 + N1, N2:2 * N2]
                p = (x_re * x_re + x_im * x_im) * isig_ref[2 * t + d]
                acc = p if acc is None else acc + p
            out_ref[s, pl.ds(t, 1), :] = jnp.max(acc, axis=0, keepdims=True)
        return carry

    lax.fori_loop(0, sidx_ref.shape[0] * n_tb, step, 0)


def run_search(sidx, isig, strain, tmpl, weights, tables):
    m1, m2, tc, ts = tables
    n_s = sidx.shape[0]
    n_t = tmpl.shape[0]
    n_tb = n_t // TB
    vmem = pltpu.VMEM
    smem = pltpu.SMEM
    ffts = n_s * n_t * 2
    cost = pl.CostEstimate(
        flops=ffts * 2 * (2 * 256 * 256 * 128),
        transcendentals=0,
        bytes_accessed=strain.size * 2 + tmpl.size * 2 + weights.size * 4,
    )
    out = pl.pallas_call(
        functools.partial(search_kernel, n_tb),
        out_shape=jax.ShapeDtypeStruct((n_s, n_t, N2), jnp.float32),
        in_specs=[pl.BlockSpec(memory_space=smem), pl.BlockSpec(memory_space=smem)]
        + [pl.BlockSpec(memory_space=vmem)] * 7,
        out_specs=pl.BlockSpec(memory_space=vmem),
        scratch_shapes=[
            pltpu.VMEM((2 * N1, 2 * TB * N2), jnp.bfloat16),
            pltpu.VMEM((2 * N1, 2 * TB * N2), jnp.float32),
            pltpu.VMEM((2 * TB * N1, 2 * N2), jnp.bfloat16),
        ],
        cost_estimate=cost,
    )(sidx, isig, strain, tmpl, weights, m1, m2, tc, ts)
    return jnp.max(out, axis=-1)


def swapped(x, axes, size, k):
    return lax.ppermute(x, axes, [(i, i ^ k) for i in range(size)])


def body(strain, templates, psd, flags, assign):
    ya = lax.axis_index("ya")
    n_ya = lax.axis_size("ya")
    n_xh = lax.axis_size("xh")
    n_yb = lax.axis_size("yb")
    n_g = n_xh * n_yb
    g = lax.axis_index("xh") * n_yb + lax.axis_index("yb")

    rows_here = psd.shape[1]
    gathered = jnp.transpose(psd, (1, 0, 2)).reshape(rows_here, -1)
    for axis in ("sc", "sz", "sx"):
        gathered = lax.all_gather(gathered, axis, axis=0, tiled=True)
    gathered, strain, templates = lax.optimization_barrier((gathered, strain, templates))
    full_psd = jnp.transpose(gathered.reshape(-1, 2, N2), (1, 0, 2))
    weights = 1.0 / full_psd
    tables = make_tables()

    tmpl_rel = jnp.concatenate(
        [templates] + [swapped(templates, ("xh", "yb"), n_g, k) for k in range(1, n_g)], 0
    )
    piece = jnp.concatenate([swapped(strain, "ya", n_ya, k) for k in range(1, n_ya)], 0)
    sigma2 = jax.vmap(lambda tmpl: template_norm(tmpl, weights))(tmpl_rel)
    isig = (1.0 / sigma2).reshape(-1)

    own_count = strain.shape[0]
    own_idx = jnp.arange(own_count, dtype=jnp.int32)
    own_rows = run_search(own_idx, isig, strain, tmpl_rel, weights, tables)
    own_rows, piece = lax.optimization_barrier((own_rows, piece))
    other_idx = jnp.arange(piece.shape[0], dtype=jnp.int32)
    other_rows = run_search(other_idx, isig, piece, tmpl_rel, weights, tables)
    slots = jnp.concatenate([own_rows, other_rows], 0).reshape(n_ya, own_count, -1)

    got1 = swapped(slots[2:4], "ya", n_ya, 2)
    got2 = swapped(jnp.stack([slots[1], got1[1]], 0), "ya", n_ya, 1)
    blocks = jnp.stack([slots[0], got1[0], got2[0], got2[1]], 0)
    blocks = blocks.reshape(n_ya, own_count, n_g, -1)
    order = jnp.array([0, 2, 1, 3], dtype=jnp.int32)
    lanes = jnp.arange(n_ya, dtype=jnp.int32)
    src_c = jnp.take(order, ya ^ lanes)
    src_t = g ^ jnp.arange(n_g, dtype=jnp.int32)
    ordered = jnp.take(jnp.take(blocks, src_c, axis=0), src_t, axis=2)
    ordered = ordered.reshape(n_ya, own_count, n_xh, n_yb, -1)
    rho2 = jnp.transpose(ordered, (1, 2, 0, 3, 4)).reshape(own_count, -1)

    peak = jnp.sqrt(rho2) * flags.astype(jnp.float32)[:, None]
    onehot = assign[:, None] == jnp.arange(BLOCKS, dtype=jnp.int32)[None, :]
    best = jnp.max(jnp.where(onehot[None], peak[:, :, None], jnp.float32(0.0)), axis=1)
    return (peak, best)


def solution(mesh):
    n_seg, n_tpl = mesh.devices.shape
    n_y = 8
    n_xh = n_tpl // n_y
    n_sz = 8
    n_sx = n_seg // (n_sz * 2)
    sub = Mesh(
        mesh.devices.reshape(n_sx, n_sz, 2, n_xh, n_y // 2, 2),
        ("sx", "sz", "sc", "xh", "ya", "yb"),
    )
    seg = ("sx", "sz", "sc")
    rows = seg + ("xh", "ya", "yb")
    placed = (
        P(rows, None, None, None, None),
        P(("xh", "ya", "yb"), None, None, None),
        P(None, seg, None),
        P(rows),
        P(),
    )
    return jax.shard_map(
        body,
        mesh=sub,
        in_specs=placed,
        out_specs=(P(rows, None), P(rows, None)),
        check_vma=False,
    )
```

```python
import functools
import math

import jax
import jax.numpy as jnp
from jax import lax
from jax.experimental import pallas as pl
from jax.experimental.pallas import tpu as pltpu
from jax.sharding import Mesh
from jax.sharding import PartitionSpec as P

N1 = 128
N2 = 128
BINS = 16384
BLOCKS = 8
TB = 4


def make_tables():
    row_idx = jnp.arange(N1, dtype=jnp.int32)
    col_idx = jnp.arange(N2, dtype=jnp.int32)
    ang_one = 2.0 * math.pi * (row_idx[:, None] * row_idx[None, :] % N1).astype(jnp.float32) / N1
    cos_one, sin_one = (jnp.cos(ang_one), jnp.sin(ang_one))
    first = jnp.concatenate(
        [jnp.concatenate([cos_one, -sin_one], 1), jnp.concatenate([sin_one, cos_one], 1)], 0
    ).astype(jnp.bfloat16)
    ang_two = 2.0 * math.pi * (col_idx[:, None] * col_idx[None, :] % N2).astype(jnp.float32) / N2
    cos_two, sin_two = (jnp.cos(ang_two), jnp.sin(ang_two))
    second = jnp.concatenate(
        [jnp.concatenate([cos_two, sin_two], 1), jnp.concatenate([-sin_two, cos_two], 1)], 0
    ).astype(jnp.bfloat16)
    ang_tw = 2.0 * math.pi * (row_idx[:, None] * col_idx[None, :] % BINS).astype(jnp.float32) / BINS
    return (first, second, jnp.cos(ang_tw), jnp.sin(ang_tw))


def template_norm(tmpl, weights):
    h_re = tmpl[0].astype(jnp.float32)
    h_im = tmpl[1].astype(jnp.float32)
    return jnp.sum((h_re * h_re + h_im * h_im) * weights, axis=(1, 2))


def search_kernel(n_tb, sidx_ref, isig_ref, strain_ref, tmpl_ref, w_ref, m1_ref, m2_ref,
                  tc_ref, ts_ref, out_ref, q_ref, y_ref, z_ref):
    nb = 2 * TB

    def step(i, carry):
        s = i // n_tb
        tb = i % n_tb
        seg = sidx_ref[s]
        for k in range(TB):
            t = tb * TB + k
            h_re = tmpl_ref[t, 0].astype(jnp.float32)
            h_im = tmpl_ref[t, 1].astype(jnp.float32)
            for d in range(2):
                d_re = strain_ref[seg, d, 0].astype(jnp.float32)
                d_im = strain_ref[seg, d, 1].astype(jnp.float32)
                w = w_ref[d]
                q_re = (d_re * h_re + d_im * h_im) * w
                q_im = (d_im * h_re - d_re * h_im) * w
                col = (2 * k + d) * N2
                q_ref[0:N1, col:col + N2] = q_re.astype(jnp.bfloat16)
                q_ref[N1:2 * N1, col:col + N2] = q_im.astype(jnp.bfloat16)
        y_ref[...] = jnp.dot(m1_ref[...], q_ref[...], preferred_element_type=jnp.float32)
        tc = tc_ref[...]
        ts = ts_ref[...]
        for b in range(nb):
            col = b * N2
            y_re = y_ref[0:N1, col:col + N2]
            y_im = y_ref[N1:2 * N1, col:col + N2]
            z_re = y_re * tc - y_im * ts
            z_im = y_re * ts + y_im * tc
            z_ref[col:col + N2, 0:N2] = z_re.astype(jnp.bfloat16)
            z_ref[col:col + N2, N2:2 * N2] = z_im.astype(jnp.bfloat16)
        x = jnp.dot(z_ref[...], m2_ref[...], preferred_element_type=jnp.float32)
        for k in range(TB):
            t = tb * TB + k
            acc = None
            for d in range(2):
                r0 = (2 * k + d) * N1
                x_re = x[r0:r0 + N1, 0:N2]
                x_im = x[r0:r0 + N1, N2:2 * N2]
                p = (x_re * x_re + x_im * x_im) * isig_ref[2 * t + d]
                acc = p if acc is None else acc + p
            out_ref[s, pl.ds(t, 1), :] = jnp.max(acc, axis=0, keepdims=True)
        return carry

    lax.fori_loop(0, sidx_ref.shape[0] * n_tb, step, 0)


def run_search(sidx, isig, strain, tmpl, weights, tables):
    m1, m2, tc, ts = tables
    n_s = sidx.shape[0]
    n_t = tmpl.shape[0]
    n_tb = n_t // TB
    vmem = pltpu.VMEM
    smem = pltpu.SMEM
    ffts = n_s * n_t * 2
    cost = pl.CostEstimate(
        flops=ffts * 2 * (2 * 256 * 256 * 128),
        transcendentals=0,
        bytes_accessed=strain.size * 2 + tmpl.size * 2 + weights.size * 4,
    )
    out = pl.pallas_call(
        functools.partial(search_kernel, n_tb),
        out_shape=jax.ShapeDtypeStruct((n_s, n_t, N2), jnp.float32),
        in_specs=[pl.BlockSpec(memory_space=smem), pl.BlockSpec(memory_space=smem)]
        + [pl.BlockSpec(memory_space=vmem)] * 7,
        out_specs=pl.BlockSpec(memory_space=vmem),
        scratch_shapes=[
            pltpu.VMEM((2 * N1, 2 * TB * N2), jnp.bfloat16),
            pltpu.VMEM((2 * N1, 2 * TB * N2), jnp.float32),
            pltpu.VMEM((2 * TB * N1, 2 * N2), jnp.bfloat16),
        ],
        cost_estimate=cost,
    )(sidx, isig, strain, tmpl, weights, m1, m2, tc, ts)
    return jnp.max(out, axis=-1)


def swapped(x, axes, size, k):
    return lax.ppermute(x, axes, [(i, i ^ k) for i in range(size)])


def body(strain, templates, psd, flags, assign):
    ya = lax.axis_index("ya")
    n_ya = lax.axis_size("ya")
    n_xh = lax.axis_size("xh")
    n_yb = lax.axis_size("yb")
    n_g = n_xh * n_yb
    g = lax.axis_index("xh") * n_yb + lax.axis_index("yb")

    rows_here = psd.shape[1]
    gathered = jnp.transpose(psd, (1, 0, 2)).reshape(rows_here, -1)
    for axis in ("sc", "sz", "sx"):
        size = lax.axis_size(axis)
        here = lax.axis_index(axis)
        bit = 1
        while bit < size:
            other = swapped(gathered, axis, size, bit)
            low = (here & bit) == 0
            gathered = jnp.where(
                low,
                jnp.concatenate([gathered, other], 0),
                jnp.concatenate([other, gathered], 0),
            )
            bit *= 2
    gathered, strain, templates = lax.optimization_barrier((gathered, strain, templates))
    full_psd = jnp.transpose(gathered.reshape(-1, 2, N2), (1, 0, 2))
    weights = 1.0 / full_psd
    tables = make_tables()

    tmpl_rel = jnp.concatenate(
        [templates] + [swapped(templates, ("xh", "yb"), n_g, k) for k in range(1, n_g)], 0
    )
    piece = jnp.concatenate([swapped(strain, "ya", n_ya, k) for k in range(1, n_ya)], 0)
    sigma2 = jax.vmap(lambda tmpl: template_norm(tmpl, weights))(tmpl_rel)
    isig = (1.0 / sigma2).reshape(-1)

    own_count = strain.shape[0]
    own_idx = jnp.arange(own_count, dtype=jnp.int32)
    own_rows = run_search(own_idx, isig, strain, tmpl_rel, weights, tables)
    own_rows, piece = lax.optimization_barrier((own_rows, piece))
    other_idx = jnp.arange(piece.shape[0], dtype=jnp.int32)
    other_rows = run_search(other_idx, isig, piece, tmpl_rel, weights, tables)
    slots = jnp.concatenate([own_rows, other_rows], 0).reshape(n_ya, own_count, -1)

    got1 = swapped(slots[2:4], "ya", n_ya, 2)
    got2 = swapped(jnp.stack([slots[1], got1[1]], 0), "ya", n_ya, 1)
    blocks = jnp.stack([slots[0], got1[0], got2[0], got2[1]], 0)
    blocks = blocks.reshape(n_ya, own_count, n_g, -1)
    order = jnp.array([0, 2, 1, 3], dtype=jnp.int32)
    lanes = jnp.arange(n_ya, dtype=jnp.int32)
    src_c = jnp.take(order, ya ^ lanes)
    src_t = g ^ jnp.arange(n_g, dtype=jnp.int32)
    ordered = jnp.take(jnp.take(blocks, src_c, axis=0), src_t, axis=2)
    ordered = ordered.reshape(n_ya, own_count, n_xh, n_yb, -1)
    rho2 = jnp.transpose(ordered, (1, 2, 0, 3, 4)).reshape(own_count, -1)

    peak = jnp.sqrt(rho2) * flags.astype(jnp.float32)[:, None]
    onehot = assign[:, None] == jnp.arange(BLOCKS, dtype=jnp.int32)[None, :]
    best = jnp.max(jnp.where(onehot[None], peak[:, :, None], jnp.float32(0.0)), axis=1)
    return (peak, best)


def solution(mesh):
    n_seg, n_tpl = mesh.devices.shape
    n_y = 8
    n_xh = n_tpl // n_y
    n_sz = 8
    n_sx = n_seg // (n_sz * 2)
    sub = Mesh(
        mesh.devices.reshape(n_sx, n_sz, 2, n_xh, n_y // 2, 2),
        ("sx", "sz", "sc", "xh", "ya", "yb"),
    )
    seg = ("sx", "sz", "sc")
    rows = seg + ("xh", "ya", "yb")
    placed = (
        P(rows, None, None, None, None),
        P(("xh", "ya", "yb"), None, None, None),
        P(None, seg, None),
        P(rows),
        P(),
    )
    return jax.shard_map(
        body,
        mesh=sub,
        in_specs=placed,
        out_specs=(P(rows, None), P(rows, None)),
        check_vma=False,
    )
```

```python
import functools
import math

import jax
import jax.numpy as jnp
from jax import lax
from jax.experimental import pallas as pl
from jax.experimental.pallas import tpu as pltpu
from jax.sharding import Mesh
from jax.sharding import PartitionSpec as P

N1 = 128
N2 = 128
BINS = 16384
BLOCKS = 8
TB = 4


def make_tables():
    row_idx = jnp.arange(N1, dtype=jnp.int32)
    col_idx = jnp.arange(N2, dtype=jnp.int32)
    ang_one = 2.0 * math.pi * (row_idx[:, None] * row_idx[None, :] % N1).astype(jnp.float32) / N1
    cos_one, sin_one = (jnp.cos(ang_one), jnp.sin(ang_one))
    first = jnp.concatenate(
        [jnp.concatenate([cos_one, -sin_one], 1), jnp.concatenate([sin_one, cos_one], 1)], 0
    ).astype(jnp.bfloat16)
    ang_two = 2.0 * math.pi * (col_idx[:, None] * col_idx[None, :] % N2).astype(jnp.float32) / N2
    cos_two, sin_two = (jnp.cos(ang_two), jnp.sin(ang_two))
    second = jnp.concatenate(
        [jnp.concatenate([cos_two, sin_two], 1), jnp.concatenate([-sin_two, cos_two], 1)], 0
    ).astype(jnp.bfloat16)
    ang_tw = 2.0 * math.pi * (row_idx[:, None] * col_idx[None, :] % BINS).astype(jnp.float32) / BINS
    return (first, second, jnp.cos(ang_tw), jnp.sin(ang_tw))


def template_norm(tmpl, weights):
    h_re = tmpl[0].astype(jnp.float32)
    h_im = tmpl[1].astype(jnp.float32)
    return jnp.sum((h_re * h_re + h_im * h_im) * weights, axis=(1, 2))


def search_kernel(n_tb, sidx_ref, isig_ref, strain_ref, tmpl_ref, w_ref, m1_ref, m2_ref,
                  tc_ref, ts_ref, out_ref, q_ref, y_ref, z_ref):
    nb = 2 * TB

    def batch(i, slot):
        s = i // n_tb
        tb = i % n_tb
        seg = sidx_ref[s]
        for k in range(TB):
            t = tb * TB + k
            h_re = tmpl_ref[t, 0].astype(jnp.float32)
            h_im = tmpl_ref[t, 1].astype(jnp.float32)
            for d in range(2):
                d_re = strain_ref[seg, d, 0].astype(jnp.float32)
                d_im = strain_ref[seg, d, 1].astype(jnp.float32)
                w = w_ref[d]
                q_re = (d_re * h_re + d_im * h_im) * w
                q_im = (d_im * h_re - d_re * h_im) * w
                col = (2 * k + d) * N2
                q_ref[slot, 0:N1, col:col + N2] = q_re.astype(jnp.bfloat16)
                q_ref[slot, N1:2 * N1, col:col + N2] = q_im.astype(jnp.bfloat16)
        y_ref[slot] = jnp.dot(m1_ref[...], q_ref[slot], preferred_element_type=jnp.float32)
        tc = tc_ref[...]
        ts = ts_ref[...]
        for b in range(nb):
            col = b * N2
            y_re = y_ref[slot, 0:N1, col:col + N2]
            y_im = y_ref[slot, N1:2 * N1, col:col + N2]
            z_re = y_re * tc - y_im * ts
            z_im = y_re * ts + y_im * tc
            z_ref[slot, col:col + N2, 0:N2] = z_re.astype(jnp.bfloat16)
            z_ref[slot, col:col + N2, N2:2 * N2] = z_im.astype(jnp.bfloat16)
        x = jnp.dot(z_ref[slot], m2_ref[...], preferred_element_type=jnp.float32)
        for k in range(TB):
            t = tb * TB + k
            acc = None
            for d in range(2):
                r0 = (2 * k + d) * N1
                x_re = x[r0:r0 + N1, 0:N2]
                x_im = x[r0:r0 + N1, N2:2 * N2]
                p = (x_re * x_re + x_im * x_im) * isig_ref[2 * t + d]
                acc = p if acc is None else acc + p
            out_ref[s, pl.ds(t, 1), :] = jnp.max(acc, axis=0, keepdims=True)

    def step(j, carry):
        batch(2 * j, 0)
        batch(2 * j + 1, 1)
        return carry

    lax.fori_loop(0, sidx_ref.shape[0] * n_tb // 2, step, 0)


def run_search(sidx, isig, strain, tmpl, weights, tables):
    m1, m2, tc, ts = tables
    n_s = sidx.shape[0]
    n_t = tmpl.shape[0]
    n_tb = n_t // TB
    vmem = pltpu.VMEM
    smem = pltpu.SMEM
    ffts = n_s * n_t * 2
    cost = pl.CostEstimate(
        flops=ffts * 2 * (2 * 256 * 256 * 128),
        transcendentals=0,
        bytes_accessed=strain.size * 2 + tmpl.size * 2 + weights.size * 4,
    )
    out = pl.pallas_call(
        functools.partial(search_kernel, n_tb),
        out_shape=jax.ShapeDtypeStruct((n_s, n_t, N2), jnp.float32),
        in_specs=[pl.BlockSpec(memory_space=smem), pl.BlockSpec(memory_space=smem)]
        + [pl.BlockSpec(memory_space=vmem)] * 7,
        out_specs=pl.BlockSpec(memory_space=vmem),
        scratch_shapes=[
            pltpu.VMEM((2, 2 * N1, 2 * TB * N2), jnp.bfloat16),
            pltpu.VMEM((2, 2 * N1, 2 * TB * N2), jnp.float32),
            pltpu.VMEM((2, 2 * TB * N1, 2 * N2), jnp.bfloat16),
        ],
        cost_estimate=cost,
    )(sidx, isig, strain, tmpl, weights, m1, m2, tc, ts)
    return jnp.max(out, axis=-1)


def swapped(x, axes, size, k):
    return lax.ppermute(x, axes, [(i, i ^ k) for i in range(size)])


def body(strain, templates, psd, flags, assign):
    ya = lax.axis_index("ya")
    n_ya = lax.axis_size("ya")
    n_xh = lax.axis_size("xh")
    n_yb = lax.axis_size("yb")
    n_g = n_xh * n_yb
    g = lax.axis_index("xh") * n_yb + lax.axis_index("yb")

    rows_here = psd.shape[1]
    gathered = jnp.transpose(psd, (1, 0, 2)).reshape(rows_here, -1)
    for axis in ("sc", "sz", "sx"):
        gathered = lax.all_gather(gathered, axis, axis=0, tiled=True)
    gathered, strain, templates = lax.optimization_barrier((gathered, strain, templates))
    full_psd = jnp.transpose(gathered.reshape(-1, 2, N2), (1, 0, 2))
    weights = 1.0 / full_psd
    tables = make_tables()

    tmpl_rel = jnp.concatenate(
        [templates] + [swapped(templates, ("xh", "yb"), n_g, k) for k in range(1, n_g)], 0
    )
    piece = jnp.concatenate([swapped(strain, "ya", n_ya, k) for k in range(1, n_ya)], 0)
    sigma2 = jax.vmap(lambda tmpl: template_norm(tmpl, weights))(tmpl_rel)
    isig = (1.0 / sigma2).reshape(-1)

    own_count = strain.shape[0]
    own_idx = jnp.arange(own_count, dtype=jnp.int32)
    own_rows = run_search(own_idx, isig, strain, tmpl_rel, weights, tables)
    own_rows, piece = lax.optimization_barrier((own_rows, piece))
    other_idx = jnp.arange(piece.shape[0], dtype=jnp.int32)
    other_rows = run_search(other_idx, isig, piece, tmpl_rel, weights, tables)
    slots = jnp.concatenate([own_rows, other_rows], 0).reshape(n_ya, own_count, -1)

    lanes = jnp.arange(n_ya, dtype=jnp.int32)
    grouped = jnp.take(slots, ya ^ lanes, axis=0)
    blocks = lax.all_to_all(grouped, "ya", split_axis=0, concat_axis=0, tiled=True)
    blocks = blocks.reshape(n_ya, own_count, n_g, -1)
    src_t = g ^ jnp.arange(n_g, dtype=jnp.int32)
    ordered = jnp.take(blocks, src_t, axis=2)
    ordered = ordered.reshape(n_ya, own_count, n_xh, n_yb, -1)
    rho2 = jnp.transpose(ordered, (1, 2, 0, 3, 4)).reshape(own_count, -1)

    peak = jnp.sqrt(rho2) * flags.astype(jnp.float32)[:, None]
    onehot = assign[:, None] == jnp.arange(BLOCKS, dtype=jnp.int32)[None, :]
    best = jnp.max(jnp.where(onehot[None], peak[:, :, None], jnp.float32(0.0)), axis=1)
    return (peak, best)


def solution(mesh):
    n_seg, n_tpl = mesh.devices.shape
    n_y = 8
    n_xh = n_tpl // n_y
    n_sz = 8
    n_sx = n_seg // (n_sz * 2)
    sub = Mesh(
        mesh.devices.reshape(n_sx, n_sz, 2, n_xh, n_y // 2, 2),
        ("sx", "sz", "sc", "xh", "ya", "yb"),
    )
    seg = ("sx", "sz", "sc")
    rows = seg + ("xh", "ya", "yb")
    placed = (
        P(rows, None, None, None, None),
        P(("xh", "ya", "yb"), None, None, None),
        P(None, seg, None),
        P(rows),
        P(),
    )
    return jax.shard_map(
        body,
        mesh=sub,
        in_specs=placed,
        out_specs=(P(rows, None), P(rows, None)),
        check_vma=False,
    )
```

```python
import functools
import math

import jax
import jax.numpy as jnp
from jax import lax
from jax.experimental import pallas as pl
from jax.experimental.pallas import tpu as pltpu
from jax.sharding import Mesh
from jax.sharding import PartitionSpec as P

N1 = 128
N2 = 128
BINS = 16384
BLOCKS = 8
TB = 4


def make_tables():
    row_idx = jnp.arange(N1, dtype=jnp.int32)
    col_idx = jnp.arange(N2, dtype=jnp.int32)
    ang_one = 2.0 * math.pi * (row_idx[:, None] * row_idx[None, :] % N1).astype(jnp.float32) / N1
    cos_one, sin_one = (jnp.cos(ang_one), jnp.sin(ang_one))
    first = jnp.concatenate(
        [jnp.concatenate([cos_one, -sin_one], 1), jnp.concatenate([sin_one, cos_one], 1)], 0
    ).astype(jnp.bfloat16)
    ang_two = 2.0 * math.pi * (col_idx[:, None] * col_idx[None, :] % N2).astype(jnp.float32) / N2
    cos_two, sin_two = (jnp.cos(ang_two), jnp.sin(ang_two))
    second = jnp.concatenate(
        [jnp.concatenate([cos_two, sin_two], 1), jnp.concatenate([-sin_two, cos_two], 1)], 0
    ).astype(jnp.bfloat16)
    ang_tw = 2.0 * math.pi * (row_idx[:, None] * col_idx[None, :] % BINS).astype(jnp.float32) / BINS
    return (first, second, jnp.cos(ang_tw), jnp.sin(ang_tw))


def template_norm(tmpl, weights):
    h_re = tmpl[0].astype(jnp.float32)
    h_im = tmpl[1].astype(jnp.float32)
    return jnp.sum((h_re * h_re + h_im * h_im) * weights, axis=(1, 2))


def search_kernel(n_tb, sidx_ref, isig_ref, strain_ref, tmpl_ref, w_ref, m1_ref, m2_ref,
                  tc_ref, ts_ref, out_ref, q_ref, y_ref, z_ref, hw_ref, sd_ref):
    nb = 2 * TB

    def weigh(t, carry):
        h_re = tmpl_ref[t, 0].astype(jnp.float32)
        h_im = tmpl_ref[t, 1].astype(jnp.float32)
        for d in range(2):
            w = w_ref[d]
            hw_ref[t, d, 0] = h_re * w
            hw_ref[t, d, 1] = h_im * w
        return carry

    lax.fori_loop(0, tmpl_ref.shape[0], weigh, 0)

    def batch(i, slot):
        s = i // n_tb
        tb = i % n_tb
        for k in range(TB):
            t = tb * TB + k
            for d in range(2):
                d_re = sd_ref[d, 0]
                d_im = sd_ref[d, 1]
                hw_re = hw_ref[t, d, 0]
                hw_im = hw_ref[t, d, 1]
                q_re = d_re * hw_re + d_im * hw_im
                q_im = d_im * hw_re - d_re * hw_im
                col = (2 * k + d) * N2
                q_ref[slot, 0:N1, col:col + N2] = q_re.astype(jnp.bfloat16)
                q_ref[slot, N1:2 * N1, col:col + N2] = q_im.astype(jnp.bfloat16)
        y_ref[slot] = jnp.dot(m1_ref[...], q_ref[slot], preferred_element_type=jnp.float32)
        tc = tc_ref[...]
        ts = ts_ref[...]
        for b in range(nb):
            col = b * N2
            y_re = y_ref[slot, 0:N1, col:col + N2]
            y_im = y_ref[slot, N1:2 * N1, col:col + N2]
            z_re = y_re * tc - y_im * ts
            z_im = y_re * ts + y_im * tc
            z_ref[slot, col:col + N2, 0:N2] = z_re.astype(jnp.bfloat16)
            z_ref[slot, col:col + N2, N2:2 * N2] = z_im.astype(jnp.bfloat16)
        x = jnp.dot(z_ref[slot], m2_ref[...], preferred_element_type=jnp.float32)
        for k in range(TB):
            t = tb * TB + k
            acc = None
            for d in range(2):
                r0 = (2 * k + d) * N1
                x_re = x[r0:r0 + N1, 0:N2]
                x_im = x[r0:r0 + N1, N2:2 * N2]
                p = (x_re * x_re + x_im * x_im) * isig_ref[2 * t + d]
                acc = p if acc is None else acc + p
            out_ref[s, pl.ds(t, 1), :] = jnp.max(acc, axis=0, keepdims=True)

    def step(j, carry):
        i = 2 * j

        @pl.when(i % n_tb == 0)
        def _():
            seg = sidx_ref[i // n_tb]
            for d in range(2):
                for part in range(2):
                    sd_ref[d, part] = strain_ref[seg, d, part].astype(jnp.float32)

        batch(i, 0)
        batch(i + 1, 1)
        return carry

    lax.fori_loop(0, sidx_ref.shape[0] * n_tb // 2, step, 0)


def run_search(sidx, isig, strain, tmpl, weights, tables):
    m1, m2, tc, ts = tables
    n_s = sidx.shape[0]
    n_t = tmpl.shape[0]
    n_tb = n_t // TB
    vmem = pltpu.VMEM
    smem = pltpu.SMEM
    ffts = n_s * n_t * 2
    cost = pl.CostEstimate(
        flops=ffts * 2 * (2 * 256 * 256 * 128),
        transcendentals=0,
        bytes_accessed=strain.size * 2 + tmpl.size * 2 + weights.size * 4,
    )
    out = pl.pallas_call(
        functools.partial(search_kernel, n_tb),
        out_shape=jax.ShapeDtypeStruct((n_s, n_t, N2), jnp.float32),
        in_specs=[pl.BlockSpec(memory_space=smem), pl.BlockSpec(memory_space=smem)]
        + [pl.BlockSpec(memory_space=vmem)] * 7,
        out_specs=pl.BlockSpec(memory_space=vmem),
        scratch_shapes=[
            pltpu.VMEM((2, 2 * N1, 2 * TB * N2), jnp.bfloat16),
            pltpu.VMEM((2, 2 * N1, 2 * TB * N2), jnp.float32),
            pltpu.VMEM((2, 2 * TB * N1, 2 * N2), jnp.bfloat16),
            pltpu.VMEM((n_t, 2, 2, N1, N2), jnp.float32),
            pltpu.VMEM((2, 2, N1, N2), jnp.float32),
        ],
        cost_estimate=cost,
    )(sidx, isig, strain, tmpl, weights, m1, m2, tc, ts)
    return jnp.max(out, axis=-1)


def swapped(x, axes, size, k):
    return lax.ppermute(x, axes, [(i, i ^ k) for i in range(size)])


def body(strain, templates, psd, flags, assign):
    ya = lax.axis_index("ya")
    n_ya = lax.axis_size("ya")
    n_xh = lax.axis_size("xh")
    n_yb = lax.axis_size("yb")
    n_g = n_xh * n_yb
    g = lax.axis_index("xh") * n_yb + lax.axis_index("yb")

    rows_here = psd.shape[1]
    gathered = jnp.transpose(psd, (1, 0, 2)).reshape(rows_here, -1)
    for axis in ("sc", "zl", "zh", "sx"):
        gathered = lax.all_gather(gathered, axis, axis=0, tiled=True)
    gathered, strain, templates = lax.optimization_barrier((gathered, strain, templates))
    full_psd = jnp.transpose(gathered.reshape(-1, 2, N2), (1, 0, 2))
    weights = 1.0 / full_psd
    tables = make_tables()

    tmpl_rel = jnp.concatenate(
        [templates] + [swapped(templates, ("xh", "yb"), n_g, k) for k in range(1, n_g)], 0
    )
    piece = jnp.concatenate([swapped(strain, "ya", n_ya, k) for k in range(1, n_ya)], 0)
    sigma2 = jax.vmap(lambda tmpl: template_norm(tmpl, weights))(tmpl_rel)
    isig = (1.0 / sigma2).reshape(-1)

    own_count = strain.shape[0]
    own_idx = jnp.arange(own_count, dtype=jnp.int32)
    own_rows = run_search(own_idx, isig, strain, tmpl_rel, weights, tables)
    own_rows, piece = lax.optimization_barrier((own_rows, piece))
    other_idx = jnp.arange(piece.shape[0], dtype=jnp.int32)
    other_rows = run_search(other_idx, isig, piece, tmpl_rel, weights, tables)
    slots = jnp.concatenate([own_rows, other_rows], 0).reshape(n_ya, own_count, -1)

    lanes = jnp.arange(n_ya, dtype=jnp.int32)
    grouped = jnp.take(slots, ya ^ lanes, axis=0)
    blocks = lax.all_to_all(grouped, "ya", split_axis=0, concat_axis=0, tiled=True)
    blocks = blocks.reshape(n_ya, own_count, n_g, -1)
    src_t = g ^ jnp.arange(n_g, dtype=jnp.int32)
    ordered = jnp.take(blocks, src_t, axis=2)
    ordered = ordered.reshape(n_ya, own_count, n_xh, n_yb, -1)
    rho2 = jnp.transpose(ordered, (1, 2, 0, 3, 4)).reshape(own_count, -1)

    peak = jnp.sqrt(rho2) * flags.astype(jnp.float32)[:, None]
    onehot = assign[:, None] == jnp.arange(BLOCKS, dtype=jnp.int32)[None, :]
    best = jnp.max(jnp.where(onehot[None], peak[:, :, None], jnp.float32(0.0)), axis=1)
    return (peak, best)


def solution(mesh):
    n_seg, n_tpl = mesh.devices.shape
    n_y = 8
    n_xh = n_tpl // n_y
    n_zl = 4
    n_zh = 2
    n_sx = n_seg // (n_zh * n_zl * 2)
    sub = Mesh(
        mesh.devices.reshape(n_sx, n_zh, n_zl, 2, n_xh, n_y // 2, 2),
        ("sx", "zh", "zl", "sc", "xh", "ya", "yb"),
    )
    seg = ("sx", "zh", "zl", "sc")
    rows = seg + ("xh", "ya", "yb")
    placed = (
        P(rows, None, None, None, None),
        P(("xh", "ya", "yb"), None, None, None),
        P(None, seg, None),
        P(rows),
        P(),
    )
    return jax.shard_map(
        body,
        mesh=sub,
        in_specs=placed,
        out_specs=(P(rows, None), P(rows, None)),
        check_vma=False,
    )
```

```python
import functools
import math

import jax
import numpy as np
import jax.numpy as jnp
from jax import lax
from jax.experimental import pallas as pl
from jax.experimental.pallas import tpu as pltpu
from jax.sharding import Mesh
from jax.sharding import PartitionSpec as P

N1 = 128
N2 = 128
BINS = 16384
BLOCKS = 8
TB = 4


def make_tables():
    f32 = np.float32
    row_idx = np.arange(N1, dtype=np.int32)
    col_idx = np.arange(N2, dtype=np.int32)

    def angle(prod, n):
        return (f32(2.0 * math.pi) * (prod % n).astype(f32)) / f32(n)

    ang_one = angle(row_idx[:, None] * row_idx[None, :], N1)
    cos_one = np.cos(ang_one.astype(np.float64)).astype(f32)
    sin_one = np.sin(ang_one.astype(np.float64)).astype(f32)
    first = np.concatenate(
        [np.concatenate([cos_one, -sin_one], 1), np.concatenate([sin_one, cos_one], 1)], 0
    )
    ang_two = angle(col_idx[:, None] * col_idx[None, :], N2)
    cos_two = np.cos(ang_two.astype(np.float64)).astype(f32)
    sin_two = np.sin(ang_two.astype(np.float64)).astype(f32)
    second = np.concatenate(
        [np.concatenate([cos_two, sin_two], 1), np.concatenate([-sin_two, cos_two], 1)], 0
    )
    ang_tw = angle(row_idx[:, None] * col_idx[None, :], BINS)
    tw_cos = np.cos(ang_tw.astype(np.float64)).astype(f32)
    tw_sin = np.sin(ang_tw.astype(np.float64)).astype(f32)
    return (
        jnp.asarray(first, dtype=jnp.bfloat16),
        jnp.asarray(second, dtype=jnp.bfloat16),
        jnp.asarray(tw_cos),
        jnp.asarray(tw_sin),
    )


def template_norm(tmpl, weights):
    h_re = tmpl[0].astype(jnp.float32)
    h_im = tmpl[1].astype(jnp.float32)
    return jnp.sum((h_re * h_re + h_im * h_im) * weights, axis=(1, 2))


def search_kernel(n_tb, sidx_ref, isig_ref, strain_ref, tmpl_ref, w_ref, m1_ref, m2_ref,
                  tc_ref, ts_ref, out_ref, q_ref, y_ref, z_ref, hw_ref, sd_ref):
    nb = 2 * TB

    def weigh(t, carry):
        h_re = tmpl_ref[t, 0].astype(jnp.float32)
        h_im = tmpl_ref[t, 1].astype(jnp.float32)
        for d in range(2):
            w = w_ref[d]
            hw_ref[t, d, 0] = h_re * w
            hw_ref[t, d, 1] = h_im * w
        return carry

    lax.fori_loop(0, tmpl_ref.shape[0], weigh, 0)

    def batch(i, slot):
        s = i // n_tb
        tb = i % n_tb
        for k in range(TB):
            t = tb * TB + k
            for d in range(2):
                d_re = sd_ref[d, 0]
                d_im = sd_ref[d, 1]
                hw_re = hw_ref[t, d, 0]
                hw_im = hw_ref[t, d, 1]
                q_re = d_re * hw_re + d_im * hw_im
                q_im = d_im * hw_re - d_re * hw_im
                col = (2 * k + d) * N2
                q_ref[slot, 0:N1, col:col + N2] = q_re.astype(jnp.bfloat16)
                q_ref[slot, N1:2 * N1, col:col + N2] = q_im.astype(jnp.bfloat16)
        y_ref[slot] = jnp.dot(m1_ref[...], q_ref[slot], preferred_element_type=jnp.float32)
        tc = tc_ref[...]
        ts = ts_ref[...]
        for b in range(nb):
            col = b * N2
            y_re = y_ref[slot, 0:N1, col:col + N2]
            y_im = y_ref[slot, N1:2 * N1, col:col + N2]
            z_re = y_re * tc - y_im * ts
            z_im = y_re * ts + y_im * tc
            z_ref[slot, col:col + N2, 0:N2] = z_re.astype(jnp.bfloat16)
            z_ref[slot, col:col + N2, N2:2 * N2] = z_im.astype(jnp.bfloat16)
        x = jnp.dot(z_ref[slot], m2_ref[...], preferred_element_type=jnp.float32)
        for k in range(TB):
            t = tb * TB + k
            acc = None
            for d in range(2):
                r0 = (2 * k + d) * N1
                x_re = x[r0:r0 + N1, 0:N2]
                x_im = x[r0:r0 + N1, N2:2 * N2]
                p = (x_re * x_re + x_im * x_im) * isig_ref[2 * t + d]
                acc = p if acc is None else acc + p
            out_ref[s, pl.ds(t, 1), :] = jnp.max(acc, axis=0, keepdims=True)

    def step(j, carry):
        i = 2 * j

        @pl.when(i % n_tb == 0)
        def _():
            seg = sidx_ref[i // n_tb]
            for d in range(2):
                for part in range(2):
                    sd_ref[d, part] = strain_ref[seg, d, part].astype(jnp.float32)

        batch(i, 0)
        batch(i + 1, 1)
        return carry

    lax.fori_loop(0, sidx_ref.shape[0] * n_tb // 2, step, 0)


def run_search(sidx, isig, strain, tmpl, weights, tables):
    m1, m2, tc, ts = tables
    n_s = sidx.shape[0]
    n_t = tmpl.shape[0]
    n_tb = n_t // TB
    vmem = pltpu.VMEM
    smem = pltpu.SMEM
    ffts = n_s * n_t * 2
    cost = pl.CostEstimate(
        flops=ffts * 2 * (2 * 256 * 256 * 128),
        transcendentals=0,
        bytes_accessed=strain.size * 2 + tmpl.size * 2 + weights.size * 4,
    )
    out = pl.pallas_call(
        functools.partial(search_kernel, n_tb),
        out_shape=jax.ShapeDtypeStruct((n_s, n_t, N2), jnp.float32),
        in_specs=[pl.BlockSpec(memory_space=smem), pl.BlockSpec(memory_space=smem)]
        + [pl.BlockSpec(memory_space=vmem)] * 7,
        out_specs=pl.BlockSpec(memory_space=vmem),
        scratch_shapes=[
            pltpu.VMEM((2, 2 * N1, 2 * TB * N2), jnp.bfloat16),
            pltpu.VMEM((2, 2 * N1, 2 * TB * N2), jnp.float32),
            pltpu.VMEM((2, 2 * TB * N1, 2 * N2), jnp.bfloat16),
            pltpu.VMEM((n_t, 2, 2, N1, N2), jnp.float32),
            pltpu.VMEM((2, 2, N1, N2), jnp.float32),
        ],
        cost_estimate=cost,
    )(sidx, isig, strain, tmpl, weights, m1, m2, tc, ts)
    return jnp.max(out, axis=-1)


def swapped(x, axes, size, k):
    return lax.ppermute(x, axes, [(i, i ^ k) for i in range(size)])


def body(strain, templates, psd, flags, assign):
    ya = lax.axis_index("ya")
    n_ya = lax.axis_size("ya")
    n_xh = lax.axis_size("xh")
    n_yb = lax.axis_size("yb")
    n_g = n_xh * n_yb
    g = lax.axis_index("xh") * n_yb + lax.axis_index("yb")

    rows_here = psd.shape[1]
    gathered = jnp.transpose(psd, (1, 0, 2)).reshape(rows_here, -1)
    for axis in ("sc", "z0", "z1", "zh", "sx"):
        gathered = lax.all_gather(gathered, axis, axis=0, tiled=True)
    gathered, strain, templates = lax.optimization_barrier((gathered, strain, templates))
    full_psd = jnp.transpose(gathered.reshape(-1, 2, N2), (1, 0, 2))
    weights = 1.0 / full_psd
    tables = make_tables()

    tmpl_rel = jnp.concatenate(
        [templates] + [swapped(templates, ("xh", "yb"), n_g, k) for k in range(1, n_g)], 0
    )
    piece = jnp.concatenate([swapped(strain, "ya", n_ya, k) for k in range(1, n_ya)], 0)
    sigma2 = jax.vmap(lambda tmpl: template_norm(tmpl, weights))(tmpl_rel)
    isig = (1.0 / sigma2).reshape(-1)

    own_count = strain.shape[0]
    own_idx = jnp.arange(own_count, dtype=jnp.int32)
    own_rows = run_search(own_idx, isig, strain, tmpl_rel, weights, tables)
    own_rows, piece = lax.optimization_barrier((own_rows, piece))
    other_idx = jnp.arange(piece.shape[0], dtype=jnp.int32)
    other_rows = run_search(other_idx, isig, piece, tmpl_rel, weights, tables)
    slots = jnp.concatenate([own_rows, other_rows], 0).reshape(n_ya, own_count, -1)

    lanes = jnp.arange(n_ya, dtype=jnp.int32)
    grouped = jnp.take(slots, ya ^ lanes, axis=0)
    blocks = lax.all_to_all(grouped, "ya", split_axis=0, concat_axis=0, tiled=True)
    blocks = blocks.reshape(n_ya, own_count, n_g, -1)
    src_t = g ^ jnp.arange(n_g, dtype=jnp.int32)
    ordered = jnp.take(blocks, src_t, axis=2)
    ordered = ordered.reshape(n_ya, own_count, n_xh, n_yb, -1)
    rho2 = jnp.transpose(ordered, (1, 2, 0, 3, 4)).reshape(own_count, -1)

    peak = jnp.sqrt(rho2) * flags.astype(jnp.float32)[:, None]
    onehot = assign[:, None] == jnp.arange(BLOCKS, dtype=jnp.int32)[None, :]
    best = jnp.max(jnp.where(onehot[None], peak[:, :, None], jnp.float32(0.0)), axis=1)
    return (peak, best)


def solution(mesh):
    n_seg, n_tpl = mesh.devices.shape
    n_y = 8
    n_xh = n_tpl // n_y
    n_zh = 2
    n_sx = n_seg // (n_zh * 2 * 2 * 2)
    sub = Mesh(
        mesh.devices.reshape(n_sx, n_zh, 2, 2, 2, n_xh, n_y // 2, 2),
        ("sx", "zh", "z1", "z0", "sc", "xh", "ya", "yb"),
    )
    seg = ("sx", "zh", "z1", "z0", "sc")
    rows = seg + ("xh", "ya", "yb")
    placed = (
        P(rows, None, None, None, None),
        P(("xh", "ya", "yb"), None, None, None),
        P(None, seg, None),
        P(rows),
        P(),
    )
    return jax.shard_map(
        body,
        mesh=sub,
        in_specs=placed,
        out_specs=(P(rows, None), P(rows, None)),
        check_vma=False,
    )
```

```python
import functools
import math

import jax
import numpy as np
import jax.numpy as jnp
from jax import lax
from jax.experimental import pallas as pl
from jax.experimental.pallas import tpu as pltpu
from jax.sharding import Mesh
from jax.sharding import PartitionSpec as P

N1 = 128
N2 = 128
BINS = 16384
BLOCKS = 8
TB = 4


def make_tables():
    f32 = np.float32
    row_idx = np.arange(N1, dtype=np.int32)
    col_idx = np.arange(N2, dtype=np.int32)

    def angle(prod, n):
        return (f32(2.0 * math.pi) * (prod % n).astype(f32)) / f32(n)

    ang_one = angle(row_idx[:, None] * row_idx[None, :], N1)
    cos_one = np.cos(ang_one.astype(np.float64)).astype(f32)
    sin_one = np.sin(ang_one.astype(np.float64)).astype(f32)
    first = np.concatenate(
        [np.concatenate([cos_one, -sin_one], 1), np.concatenate([sin_one, cos_one], 1)], 0
    )
    ang_two = angle(col_idx[:, None] * col_idx[None, :], N2)
    cos_two = np.cos(ang_two.astype(np.float64)).astype(f32)
    sin_two = np.sin(ang_two.astype(np.float64)).astype(f32)
    second = np.concatenate(
        [np.concatenate([cos_two, sin_two], 1), np.concatenate([-sin_two, cos_two], 1)], 0
    )
    ang_tw = angle(row_idx[:, None] * col_idx[None, :], BINS)
    tw_cos = np.cos(ang_tw.astype(np.float64)).astype(f32)
    tw_sin = np.sin(ang_tw.astype(np.float64)).astype(f32)
    return (
        jnp.asarray(first, dtype=jnp.bfloat16),
        jnp.asarray(second, dtype=jnp.bfloat16),
        jnp.asarray(tw_cos),
        jnp.asarray(tw_sin),
    )


def template_norm(tmpl, weights):
    h_re = tmpl[0].astype(jnp.float32)
    h_im = tmpl[1].astype(jnp.float32)
    return jnp.sum((h_re * h_re + h_im * h_im) * weights, axis=(1, 2))


def search_kernel(n_tb, sidx_ref, isig_ref, strain_ref, tmpl_ref, w_ref, m1_ref, m2_ref,
                  tc_ref, ts_ref, out_ref, q_ref, y_ref, z_ref, hw_ref, sd_ref):
    nb = 2 * TB

    def weigh(t, carry):
        h_re = tmpl_ref[t, 0].astype(jnp.float32)
        h_im = tmpl_ref[t, 1].astype(jnp.float32)
        for d in range(2):
            w = w_ref[d]
            hw_ref[t, d, 0] = h_re * w
            hw_ref[t, d, 1] = h_im * w
        return carry

    lax.fori_loop(0, tmpl_ref.shape[0], weigh, 0)

    def batch(i, slot):
        s = i // n_tb
        tb = i % n_tb
        for k in range(TB):
            t = tb * TB + k
            for d in range(2):
                d_re = sd_ref[d, 0]
                d_im = sd_ref[d, 1]
                hw_re = hw_ref[t, d, 0]
                hw_im = hw_ref[t, d, 1]
                q_re = d_re * hw_re + d_im * hw_im
                q_im = d_im * hw_re - d_re * hw_im
                col = (2 * k + d) * N2
                q_ref[slot, 0:N1, col:col + N2] = q_re.astype(jnp.bfloat16)
                q_ref[slot, N1:2 * N1, col:col + N2] = q_im.astype(jnp.bfloat16)
        y_ref[slot] = jnp.dot(m1_ref[...], q_ref[slot], preferred_element_type=jnp.float32)
        tc = tc_ref[...]
        ts = ts_ref[...]
        for b in range(nb):
            col = b * N2
            y_re = y_ref[slot, 0:N1, col:col + N2]
            y_im = y_ref[slot, N1:2 * N1, col:col + N2]
            z_re = y_re * tc - y_im * ts
            z_im = y_re * ts + y_im * tc
            z_ref[slot, col:col + N2, 0:N2] = z_re.astype(jnp.bfloat16)
            z_ref[slot, col:col + N2, N2:2 * N2] = z_im.astype(jnp.bfloat16)
        x = jnp.dot(z_ref[slot], m2_ref[...], preferred_element_type=jnp.float32)
        for k in range(TB):
            t = tb * TB + k
            acc = None
            for d in range(2):
                r0 = (2 * k + d) * N1
                x_re = x[r0:r0 + N1, 0:N2]
                x_im = x[r0:r0 + N1, N2:2 * N2]
                p = (x_re * x_re + x_im * x_im) * isig_ref[2 * t + d]
                acc = p if acc is None else acc + p
            out_ref[s, pl.ds(t, 1), :] = jnp.max(acc, axis=0, keepdims=True)

    def step(j, carry):
        i = 2 * j

        @pl.when(i % n_tb == 0)
        def _():
            seg = sidx_ref[i // n_tb]
            for d in range(2):
                for part in range(2):
                    sd_ref[d, part] = strain_ref[seg, d, part].astype(jnp.float32)

        batch(i, 0)
        batch(i + 1, 1)
        return carry

    lax.fori_loop(0, sidx_ref.shape[0] * n_tb // 2, step, 0)


def run_search(sidx, isig, strain, tmpl, weights, tables):
    m1, m2, tc, ts = tables
    n_s = sidx.shape[0]
    n_t = tmpl.shape[0]
    n_tb = n_t // TB
    vmem = pltpu.VMEM
    smem = pltpu.SMEM
    ffts = n_s * n_t * 2
    cost = pl.CostEstimate(
        flops=ffts * 2 * (2 * 256 * 256 * 128),
        transcendentals=0,
        bytes_accessed=strain.size * 2 + tmpl.size * 2 + weights.size * 4,
    )
    out = pl.pallas_call(
        functools.partial(search_kernel, n_tb),
        out_shape=jax.ShapeDtypeStruct((n_s, n_t, N2), jnp.float32),
        in_specs=[pl.BlockSpec(memory_space=smem), pl.BlockSpec(memory_space=smem)]
        + [pl.BlockSpec(memory_space=vmem)] * 7,
        out_specs=pl.BlockSpec(memory_space=vmem),
        scratch_shapes=[
            pltpu.VMEM((2, 2 * N1, 2 * TB * N2), jnp.bfloat16),
            pltpu.VMEM((2, 2 * N1, 2 * TB * N2), jnp.float32),
            pltpu.VMEM((2, 2 * TB * N1, 2 * N2), jnp.bfloat16),
            pltpu.VMEM((n_t, 2, 2, N1, N2), jnp.float32),
            pltpu.VMEM((2, 2, N1, N2), jnp.float32),
        ],
        cost_estimate=cost,
    )(sidx, isig, strain, tmpl, weights, m1, m2, tc, ts)
    return jnp.max(out, axis=-1)


def swapped(x, axes, size, k):
    return lax.ppermute(x, axes, [(i, i ^ k) for i in range(size)])


def body(strain, templates, psd, flags, assign):
    ya = lax.axis_index(("ya1", "ya0"))
    n_ya = lax.axis_size(("ya1", "ya0"))
    n_xh = lax.axis_size("xh")
    n_yb = lax.axis_size("yb")
    n_g = n_xh * n_yb
    g = lax.axis_index("xh") * n_yb + lax.axis_index("yb")

    rows_here = psd.shape[1]
    gathered = jnp.transpose(psd, (1, 0, 2)).reshape(rows_here, -1)
    for axis in ("sc", "z0", "z1", "zh", "sx"):
        gathered = lax.all_gather(gathered, axis, axis=0, tiled=True)
    gathered, strain, templates = lax.optimization_barrier((gathered, strain, templates))
    full_psd = jnp.transpose(gathered.reshape(-1, 2, N2), (1, 0, 2))
    weights = 1.0 / full_psd
    tables = make_tables()

    tmpl_rel = jnp.concatenate(
        [templates] + [swapped(templates, ("xh", "yb"), n_g, k) for k in range(1, n_g)], 0
    )
    piece = jnp.concatenate([swapped(strain, ("ya1", "ya0"), n_ya, k) for k in range(1, n_ya)], 0)
    sigma2 = jax.vmap(lambda tmpl: template_norm(tmpl, weights))(tmpl_rel)
    isig = (1.0 / sigma2).reshape(-1)

    own_count = strain.shape[0]
    own_idx = jnp.arange(own_count, dtype=jnp.int32)
    own_rows = run_search(own_idx, isig, strain, tmpl_rel, weights, tables)
    own_rows, piece = lax.optimization_barrier((own_rows, piece))
    other_idx = jnp.arange(piece.shape[0], dtype=jnp.int32)
    other_rows = run_search(other_idx, isig, piece, tmpl_rel, weights, tables)
    slots = jnp.concatenate([own_rows, other_rows], 0).reshape(n_ya, own_count, -1)

    lanes = jnp.arange(n_ya, dtype=jnp.int32)
    every = slots[None]
    for axis in ("ya0", "ya1"):
        every = lax.all_gather(every, axis, axis=0, tiled=True)
    blocks = every[lanes, ya ^ lanes]
    blocks = blocks.reshape(n_ya, own_count, n_g, -1)
    src_t = g ^ jnp.arange(n_g, dtype=jnp.int32)
    ordered = jnp.take(blocks, src_t, axis=2)
    ordered = ordered.reshape(n_ya, own_count, n_xh, n_yb, -1)
    rho2 = jnp.transpose(ordered, (1, 2, 0, 3, 4)).reshape(own_count, -1)

    peak = jnp.sqrt(rho2) * flags.astype(jnp.float32)[:, None]
    onehot = assign[:, None] == jnp.arange(BLOCKS, dtype=jnp.int32)[None, :]
    best = jnp.max(jnp.where(onehot[None], peak[:, :, None], jnp.float32(0.0)), axis=1)
    return (peak, best)


def solution(mesh):
    n_seg, n_tpl = mesh.devices.shape
    n_y = 8
    n_xh = n_tpl // n_y
    n_zh = 2
    n_sx = n_seg // (n_zh * 2 * 2 * 2)
    sub = Mesh(
        mesh.devices.reshape(n_sx, n_zh, 2, 2, 2, n_xh, 2, n_y // 4, 2),
        ("sx", "zh", "z1", "z0", "sc", "xh", "ya1", "ya0", "yb"),
    )
    seg = ("sx", "zh", "z1", "z0", "sc")
    rows = seg + ("xh", "ya1", "ya0", "yb")
    placed = (
        P(rows, None, None, None, None),
        P(("xh", "ya1", "ya0", "yb"), None, None, None),
        P(None, seg, None),
        P(rows),
        P(),
    )
    return jax.shard_map(
        body,
        mesh=sub,
        in_specs=placed,
        out_specs=(P(rows, None), P(rows, None)),
        check_vma=False,
    )
```

```python
import functools
import math

import jax
import numpy as np
import jax.numpy as jnp
from jax import lax
from jax.experimental import pallas as pl
from jax.experimental.pallas import tpu as pltpu
from jax.sharding import Mesh
from jax.sharding import PartitionSpec as P

N1 = 128
N2 = 128
BINS = 16384
BLOCKS = 8
TB = 4


def make_tables():
    f32 = np.float32
    row_idx = np.arange(N1, dtype=np.int32)
    col_idx = np.arange(N2, dtype=np.int32)

    def angle(prod, n):
        return (f32(2.0 * math.pi) * (prod % n).astype(f32)) / f32(n)

    ang_one = angle(row_idx[:, None] * row_idx[None, :], N1)
    cos_one = np.cos(ang_one.astype(np.float64)).astype(f32)
    sin_one = np.sin(ang_one.astype(np.float64)).astype(f32)
    first = np.concatenate(
        [np.concatenate([cos_one, -sin_one], 1), np.concatenate([sin_one, cos_one], 1)], 0
    )
    ang_two = angle(col_idx[:, None] * col_idx[None, :], N2)
    cos_two = np.cos(ang_two.astype(np.float64)).astype(f32)
    sin_two = np.sin(ang_two.astype(np.float64)).astype(f32)
    second = np.concatenate(
        [np.concatenate([cos_two, sin_two], 1), np.concatenate([-sin_two, cos_two], 1)], 0
    )
    ang_tw = angle(row_idx[:, None] * col_idx[None, :], BINS)
    tw_cos = np.cos(ang_tw.astype(np.float64)).astype(f32)
    tw_sin = np.sin(ang_tw.astype(np.float64)).astype(f32)
    return (
        jnp.asarray(first, dtype=jnp.bfloat16),
        jnp.asarray(second, dtype=jnp.bfloat16),
        jnp.asarray(tw_cos),
        jnp.asarray(tw_sin),
    )


def template_norm(tmpl, weights):
    h_re = tmpl[0].astype(jnp.float32)
    h_im = tmpl[1].astype(jnp.float32)
    return jnp.sum((h_re * h_re + h_im * h_im) * weights, axis=(1, 2))


def search_kernel(n_tb, isig_ref, strain_ref, tmpl_ref, w_ref, m1_ref, m2_ref,
                  tc_ref, ts_ref, out_ref, q_ref, y_ref, z_ref, hw_ref, sd_ref):
    nb = 2 * TB

    def weigh(t, carry):
        h_re = tmpl_ref[t, 0].astype(jnp.float32)
        h_im = tmpl_ref[t, 1].astype(jnp.float32)
        for d in range(2):
            w = w_ref[d]
            hw_ref[t, d, 0] = h_re * w
            hw_ref[t, d, 1] = h_im * w
        return carry

    lax.fori_loop(0, tmpl_ref.shape[0], weigh, 0)
    out_ref[...] = jnp.zeros(out_ref.shape, jnp.float32)

    def batch(i, slot):
        s = i // n_tb
        tb = i % n_tb
        for k in range(TB):
            t = tb * TB + k
            for d in range(2):
                d_re = sd_ref[d, 0]
                d_im = sd_ref[d, 1]
                hw_re = hw_ref[t, d, 0]
                hw_im = hw_ref[t, d, 1]
                q_re = d_re * hw_re + d_im * hw_im
                q_im = d_im * hw_re - d_re * hw_im
                col = (2 * k + d) * N2
                q_ref[slot, 0:N1, col:col + N2] = q_re.astype(jnp.bfloat16)
                q_ref[slot, N1:2 * N1, col:col + N2] = q_im.astype(jnp.bfloat16)
        y_ref[slot] = jnp.dot(m1_ref[...], q_ref[slot], preferred_element_type=jnp.float32)
        tc = tc_ref[...]
        ts = ts_ref[...]
        for b in range(nb):
            col = b * N2
            y_re = y_ref[slot, 0:N1, col:col + N2]
            y_im = y_ref[slot, N1:2 * N1, col:col + N2]
            z_re = y_re * tc - y_im * ts
            z_im = y_re * ts + y_im * tc
            z_ref[slot, col:col + N2, 0:N2] = z_re.astype(jnp.bfloat16)
            z_ref[slot, col:col + N2, N2:2 * N2] = z_im.astype(jnp.bfloat16)
        x = jnp.dot(z_ref[slot], m2_ref[...], preferred_element_type=jnp.float32)
        for k in range(TB):
            t = tb * TB + k
            acc = None
            for d in range(2):
                r0 = (2 * k + d) * N1
                x_re = x[r0:r0 + N1, 0:N2]
                x_im = x[r0:r0 + N1, N2:2 * N2]
                p = (x_re * x_re + x_im * x_im) * isig_ref[2 * t + d]
                acc = p if acc is None else acc + p
            best_t = jnp.max(jnp.max(acc, axis=0, keepdims=True), axis=1, keepdims=True)
            lane = lax.broadcasted_iota(jnp.int32, (1, N2), 1)
            row = out_ref[pl.ds(s, 1), :]
            out_ref[pl.ds(s, 1), :] = jnp.where(lane == t, best_t, row)

    def step(j, carry):
        i = 2 * j

        @pl.when(i % n_tb == 0)
        def _():
            seg = i // n_tb
            for d in range(2):
                for part in range(2):
                    sd_ref[d, part] = strain_ref[seg, d, part].astype(jnp.float32)

        batch(i, 0)
        batch(i + 1, 1)
        return carry

    lax.fori_loop(0, out_ref.shape[0] * n_tb // 2, step, 0)


def run_search(isig, strain, tmpl, weights, tables):
    m1, m2, tc, ts = tables
    n_s = strain.shape[0]
    n_t = tmpl.shape[0]
    n_tb = n_t // TB
    vmem = pltpu.VMEM
    smem = pltpu.SMEM
    ffts = n_s * n_t * 2
    cost = pl.CostEstimate(
        flops=ffts * 2 * (2 * 256 * 256 * 128),
        transcendentals=0,
        bytes_accessed=strain.size * 2 + tmpl.size * 2 + weights.size * 4,
    )
    out = pl.pallas_call(
        functools.partial(search_kernel, n_tb),
        out_shape=jax.ShapeDtypeStruct((n_s, N2), jnp.float32),
        in_specs=[pl.BlockSpec(memory_space=smem)] + [pl.BlockSpec(memory_space=vmem)] * 7,
        out_specs=pl.BlockSpec(memory_space=vmem),
        scratch_shapes=[
            pltpu.VMEM((2, 2 * N1, 2 * TB * N2), jnp.bfloat16),
            pltpu.VMEM((2, 2 * N1, 2 * TB * N2), jnp.float32),
            pltpu.VMEM((2, 2 * TB * N1, 2 * N2), jnp.bfloat16),
            pltpu.VMEM((n_t, 2, 2, N1, N2), jnp.float32),
            pltpu.VMEM((2, 2, N1, N2), jnp.float32),
        ],
        cost_estimate=cost,
    )(isig, strain, tmpl, weights, m1, m2, tc, ts)
    return out[:, :n_t]


def swapped(x, axes, size, k):
    return lax.ppermute(x, axes, [(i, i ^ k) for i in range(size)])


def body(strain, templates, psd, flags, assign):
    ya = lax.axis_index("ya")
    n_ya = lax.axis_size("ya")
    n_xh = lax.axis_size("xh")
    n_yb = lax.axis_size("yb")
    n_g = n_xh * n_yb
    g = lax.axis_index("xh") * n_yb + lax.axis_index("yb")

    rows_here = psd.shape[1]
    gathered = jnp.transpose(psd, (1, 0, 2)).reshape(rows_here, -1)
    for axis in ("sc", "z0", "z1", "zh", "sx"):
        gathered = lax.all_gather(gathered, axis, axis=0, tiled=True)
    gathered, strain, templates = lax.optimization_barrier((gathered, strain, templates))
    full_psd = jnp.transpose(gathered.reshape(-1, 2, N2), (1, 0, 2))
    weights = 1.0 / full_psd
    tables = make_tables()

    tmpl_rel = jnp.concatenate(
        [templates] + [swapped(templates, ("xh", "yb"), n_g, k) for k in range(1, n_g)], 0
    )
    piece = jnp.concatenate([swapped(strain, "ya", n_ya, k) for k in range(1, n_ya)], 0)
    sigma2 = jax.vmap(lambda tmpl: template_norm(tmpl, weights))(tmpl_rel)
    isig = (1.0 / sigma2).reshape(-1)

    own_count = strain.shape[0]
    own_rows = run_search(isig, strain, tmpl_rel, weights, tables)
    own_rows, piece = lax.optimization_barrier((own_rows, piece))
    other_rows = run_search(isig, piece, tmpl_rel, weights, tables)
    slots = jnp.concatenate([own_rows, other_rows], 0).reshape(n_ya, own_count, -1)

    lanes = jnp.arange(n_ya, dtype=jnp.int32)
    grouped = jnp.take(slots, ya ^ lanes, axis=0)
    blocks = lax.all_to_all(grouped, "ya", split_axis=0, concat_axis=0, tiled=True)
    blocks = blocks.reshape(n_ya, own_count, n_g, -1)
    src_t = g ^ jnp.arange(n_g, dtype=jnp.int32)
    ordered = jnp.take(blocks, src_t, axis=2)
    ordered = ordered.reshape(n_ya, own_count, n_xh, n_yb, -1)
    rho2 = jnp.transpose(ordered, (1, 2, 0, 3, 4)).reshape(own_count, -1)

    peak = jnp.sqrt(rho2) * flags.astype(jnp.float32)[:, None]
    onehot = assign[:, None] == jnp.arange(BLOCKS, dtype=jnp.int32)[None, :]
    best = jnp.max(jnp.where(onehot[None], peak[:, :, None], jnp.float32(0.0)), axis=1)
    return (peak, best)


def solution(mesh):
    n_seg, n_tpl = mesh.devices.shape
    n_y = 8
    n_xh = n_tpl // n_y
    n_zh = 2
    n_sx = n_seg // (n_zh * 2 * 2 * 2)
    sub = Mesh(
        mesh.devices.reshape(n_sx, n_zh, 2, 2, 2, n_xh, n_y // 2, 2),
        ("sx", "zh", "z1", "z0", "sc", "xh", "ya", "yb"),
    )
    seg = ("sx", "zh", "z1", "z0", "sc")
    rows = seg + ("xh", "ya", "yb")
    placed = (
        P(rows, None, None, None, None),
        P(("xh", "ya", "yb"), None, None, None),
        P(None, seg, None),
        P(rows),
        P(),
    )
    return jax.shard_map(
        body,
        mesh=sub,
        in_specs=placed,
        out_specs=(P(rows, None), P(rows, None)),
        check_vma=False,
    )
```

```python
import functools
import math

import jax
import numpy as np
import jax.numpy as jnp
from jax import lax
from jax.experimental import pallas as pl
from jax.experimental.pallas import tpu as pltpu
from jax.sharding import Mesh
from jax.sharding import PartitionSpec as P

N1 = 128
N2 = 128
BINS = 16384
BLOCKS = 8
TB = 8


def make_tables():
    f32 = np.float32
    row_idx = np.arange(N1, dtype=np.int32)
    col_idx = np.arange(N2, dtype=np.int32)

    def angle(prod, n):
        return (f32(2.0 * math.pi) * (prod % n).astype(f32)) / f32(n)

    ang_one = angle(row_idx[:, None] * row_idx[None, :], N1)
    cos_one = np.cos(ang_one.astype(np.float64)).astype(f32)
    sin_one = np.sin(ang_one.astype(np.float64)).astype(f32)
    first = np.concatenate(
        [np.concatenate([cos_one, -sin_one], 1), np.concatenate([sin_one, cos_one], 1)], 0
    )
    ang_two = angle(col_idx[:, None] * col_idx[None, :], N2)
    cos_two = np.cos(ang_two.astype(np.float64)).astype(f32)
    sin_two = np.sin(ang_two.astype(np.float64)).astype(f32)
    second = np.concatenate(
        [np.concatenate([cos_two, sin_two], 1), np.concatenate([-sin_two, cos_two], 1)], 0
    )
    ang_tw = angle(row_idx[:, None] * col_idx[None, :], BINS)
    tw_cos = np.cos(ang_tw.astype(np.float64)).astype(f32)
    tw_sin = np.sin(ang_tw.astype(np.float64)).astype(f32)
    return (
        jnp.asarray(first, dtype=jnp.bfloat16),
        jnp.asarray(second, dtype=jnp.bfloat16),
        jnp.asarray(tw_cos),
        jnp.asarray(tw_sin),
    )


def template_norm(tmpl, weights):
    h_re = tmpl[0].astype(jnp.float32)
    h_im = tmpl[1].astype(jnp.float32)
    return jnp.sum((h_re * h_re + h_im * h_im) * weights, axis=(1, 2))


def search_kernel(n_tb, isig_ref, strain_ref, tmpl_ref, w_ref, m1_ref, m2_ref,
                  tc_ref, ts_ref, out_ref, q_ref, y_ref, z_ref, hw_ref, sd_ref):
    nb = 2 * TB

    def weigh(t, carry):
        h_re = tmpl_ref[t, 0].astype(jnp.float32)
        h_im = tmpl_ref[t, 1].astype(jnp.float32)
        for d in range(2):
            w = w_ref[d]
            hw_ref[t, d, 0] = h_re * w
            hw_ref[t, d, 1] = h_im * w
        return carry

    lax.fori_loop(0, tmpl_ref.shape[0], weigh, 0)
    out_ref[...] = jnp.zeros(out_ref.shape, jnp.float32)

    def batch(i, slot):
        s = i // n_tb
        tb = i % n_tb
        for k in range(TB):
            t = tb * TB + k
            for d in range(2):
                d_re = sd_ref[d, 0]
                d_im = sd_ref[d, 1]
                hw_re = hw_ref[t, d, 0]
                hw_im = hw_ref[t, d, 1]
                q_re = d_re * hw_re + d_im * hw_im
                q_im = d_im * hw_re - d_re * hw_im
                col = (2 * k + d) * N2
                q_ref[slot, 0:N1, col:col + N2] = q_re.astype(jnp.bfloat16)
                q_ref[slot, N1:2 * N1, col:col + N2] = q_im.astype(jnp.bfloat16)
        y_ref[slot] = jnp.dot(m1_ref[...], q_ref[slot], preferred_element_type=jnp.float32)
        tc = tc_ref[...]
        ts = ts_ref[...]
        for b in range(nb):
            col = b * N2
            y_re = y_ref[slot, 0:N1, col:col + N2]
            y_im = y_ref[slot, N1:2 * N1, col:col + N2]
            z_re = y_re * tc - y_im * ts
            z_im = y_re * ts + y_im * tc
            z_ref[slot, col:col + N2, 0:N2] = z_re.astype(jnp.bfloat16)
            z_ref[slot, col:col + N2, N2:2 * N2] = z_im.astype(jnp.bfloat16)
        x = jnp.dot(z_ref[slot], m2_ref[...], preferred_element_type=jnp.float32)
        for k in range(TB):
            t = tb * TB + k
            acc = None
            for d in range(2):
                r0 = (2 * k + d) * N1
                x_re = x[r0:r0 + N1, 0:N2]
                x_im = x[r0:r0 + N1, N2:2 * N2]
                p = (x_re * x_re + x_im * x_im) * isig_ref[2 * t + d]
                acc = p if acc is None else acc + p
            best_t = jnp.max(jnp.max(acc, axis=0, keepdims=True), axis=1, keepdims=True)
            lane = lax.broadcasted_iota(jnp.int32, (1, N2), 1)
            row = out_ref[pl.ds(s, 1), :]
            out_ref[pl.ds(s, 1), :] = jnp.where(lane == t, best_t, row)

    def step(j, carry):
        i = 2 * j

        @pl.when(i % n_tb == 0)
        def _():
            seg = i // n_tb
            for d in range(2):
                for part in range(2):
                    sd_ref[d, part] = strain_ref[seg, d, part].astype(jnp.float32)

        batch(i, 0)
        batch(i + 1, 1)
        return carry

    lax.fori_loop(0, out_ref.shape[0] * n_tb // 2, step, 0)


def run_search(isig, strain, tmpl, weights, tables):
    m1, m2, tc, ts = tables
    n_s = strain.shape[0]
    n_t = tmpl.shape[0]
    n_tb = n_t // TB
    vmem = pltpu.VMEM
    smem = pltpu.SMEM
    ffts = n_s * n_t * 2
    cost = pl.CostEstimate(
        flops=ffts * 2 * (2 * 256 * 256 * 128),
        transcendentals=0,
        bytes_accessed=strain.size * 2 + tmpl.size * 2 + weights.size * 4,
    )
    out = pl.pallas_call(
        functools.partial(search_kernel, n_tb),
        out_shape=jax.ShapeDtypeStruct((n_s, N2), jnp.float32),
        in_specs=[pl.BlockSpec(memory_space=smem)] + [pl.BlockSpec(memory_space=vmem)] * 7,
        out_specs=pl.BlockSpec(memory_space=vmem),
        scratch_shapes=[
            pltpu.VMEM((2, 2 * N1, 2 * TB * N2), jnp.bfloat16),
            pltpu.VMEM((2, 2 * N1, 2 * TB * N2), jnp.float32),
            pltpu.VMEM((2, 2 * TB * N1, 2 * N2), jnp.bfloat16),
            pltpu.VMEM((n_t, 2, 2, N1, N2), jnp.float32),
            pltpu.VMEM((2, 2, N1, N2), jnp.float32),
        ],
        cost_estimate=cost,
    )(isig, strain, tmpl, weights, m1, m2, tc, ts)
    return out[:, :n_t]


def swapped(x, axes, size, k):
    return lax.ppermute(x, axes, [(i, i ^ k) for i in range(size)])


def body(strain, templates, psd, flags, assign):
    ya = lax.axis_index("ya")
    n_ya = lax.axis_size("ya")
    n_xh = lax.axis_size("xh")
    n_yb = lax.axis_size("yb")
    n_g = n_xh * n_yb
    g = lax.axis_index("xh") * n_yb + lax.axis_index("yb")

    rows_here = psd.shape[1]
    gathered = jnp.transpose(psd, (1, 0, 2)).reshape(rows_here, -1)
    for axis in ("sc", "z0", "z1", "zh", "sx"):
        gathered = lax.all_gather(gathered, axis, axis=0, tiled=True)
    gathered, strain, templates = lax.optimization_barrier((gathered, strain, templates))
    full_psd = jnp.transpose(gathered.reshape(-1, 2, N2), (1, 0, 2))
    weights = 1.0 / full_psd
    tables = make_tables()

    tmpl_rel = jnp.concatenate(
        [templates] + [swapped(templates, ("xh", "yb"), n_g, k) for k in range(1, n_g)], 0
    )
    piece = jnp.concatenate([swapped(strain, "ya", n_ya, k) for k in range(1, n_ya)], 0)
    sigma2 = jax.vmap(lambda tmpl: template_norm(tmpl, weights))(tmpl_rel)
    isig = (1.0 / sigma2).reshape(-1)

    own_count = strain.shape[0]
    own_rows = run_search(isig, strain, tmpl_rel, weights, tables)
    own_rows, piece = lax.optimization_barrier((own_rows, piece))
    other_rows = run_search(isig, piece, tmpl_rel, weights, tables)
    slots = jnp.concatenate([own_rows, other_rows], 0).reshape(n_ya, own_count, -1)

    lanes = jnp.arange(n_ya, dtype=jnp.int32)
    grouped = jnp.take(slots, ya ^ lanes, axis=0)
    blocks = lax.all_to_all(grouped, "ya", split_axis=0, concat_axis=0, tiled=True)
    blocks = blocks.reshape(n_ya, own_count, n_g, -1)
    src_t = g ^ jnp.arange(n_g, dtype=jnp.int32)
    ordered = jnp.take(blocks, src_t, axis=2)
    ordered = ordered.reshape(n_ya, own_count, n_xh, n_yb, -1)
    rho2 = jnp.transpose(ordered, (1, 2, 0, 3, 4)).reshape(own_count, -1)

    peak = jnp.sqrt(rho2) * flags.astype(jnp.float32)[:, None]
    onehot = assign[:, None] == jnp.arange(BLOCKS, dtype=jnp.int32)[None, :]
    best = jnp.max(jnp.where(onehot[None], peak[:, :, None], jnp.float32(0.0)), axis=1)
    return (peak, best)


def solution(mesh):
    n_seg, n_tpl = mesh.devices.shape
    n_y = 8
    n_xh = n_tpl // n_y
    n_zh = 2
    n_sx = n_seg // (n_zh * 2 * 2 * 2)
    sub = Mesh(
        mesh.devices.reshape(n_sx, n_zh, 2, 2, 2, n_xh, n_y // 2, 2),
        ("sx", "zh", "z1", "z0", "sc", "xh", "ya", "yb"),
    )
    seg = ("sx", "zh", "z1", "z0", "sc")
    rows = seg + ("xh", "ya", "yb")
    placed = (
        P(rows, None, None, None, None),
        P(("xh", "ya", "yb"), None, None, None),
        P(None, seg, None),
        P(rows),
        P(),
    )
    return jax.shard_map(
        body,
        mesh=sub,
        in_specs=placed,
        out_specs=(P(rows, None), P(rows, None)),
        check_vma=False,
    )
```

```python
import functools
import math

import jax
import numpy as np
import jax.numpy as jnp
from jax import lax
from jax.experimental import pallas as pl
from jax.experimental.pallas import tpu as pltpu
from jax.sharding import Mesh
from jax.sharding import PartitionSpec as P

N1 = 128
N2 = 128
BINS = 16384
BLOCKS = 8
TB = 8


def make_tables():
    f32 = np.float32
    row_idx = np.arange(N1, dtype=np.int32)
    col_idx = np.arange(N2, dtype=np.int32)

    def angle(prod, n):
        return (f32(2.0 * math.pi) * (prod % n).astype(f32)) / f32(n)

    ang_one = angle(row_idx[:, None] * row_idx[None, :], N1)
    cos_one = np.cos(ang_one.astype(np.float64)).astype(f32)
    sin_one = np.sin(ang_one.astype(np.float64)).astype(f32)
    first = np.concatenate(
        [np.concatenate([cos_one, -sin_one], 1), np.concatenate([sin_one, cos_one], 1)], 0
    )
    ang_two = angle(col_idx[:, None] * col_idx[None, :], N2)
    cos_two = np.cos(ang_two.astype(np.float64)).astype(f32)
    sin_two = np.sin(ang_two.astype(np.float64)).astype(f32)
    second = np.concatenate(
        [np.concatenate([cos_two, sin_two], 1), np.concatenate([-sin_two, cos_two], 1)], 0
    )
    ang_tw = angle(row_idx[:, None] * col_idx[None, :], BINS)
    tw_cos = np.cos(ang_tw.astype(np.float64)).astype(f32)
    tw_sin = np.sin(ang_tw.astype(np.float64)).astype(f32)
    return (
        jnp.asarray(first, dtype=jnp.bfloat16),
        jnp.asarray(second, dtype=jnp.bfloat16),
        jnp.asarray(tw_cos),
        jnp.asarray(tw_sin),
    )


def template_norm(tmpl, weights):
    h_re = tmpl[0].astype(jnp.float32)
    h_im = tmpl[1].astype(jnp.float32)
    return jnp.sum((h_re * h_re + h_im * h_im) * weights, axis=(1, 2))


def search_kernel(n_tb, isig_ref, strain_ref, tmpl_ref, w_ref, m1_ref, m2_ref,
                  tc_ref, ts_ref, out_ref, q_ref, y_ref, z_ref, hw_ref, sd_ref):
    nb = 2 * TB

    def weigh(t, carry):
        h_re = tmpl_ref[t, 0].astype(jnp.float32)
        h_im = tmpl_ref[t, 1].astype(jnp.float32)
        for d in range(2):
            w = w_ref[d]
            hw_ref[t, d, 0] = h_re * w
            hw_ref[t, d, 1] = h_im * w
        return carry

    lax.fori_loop(0, tmpl_ref.shape[0], weigh, 0)
    out_ref[...] = jnp.zeros(out_ref.shape, jnp.float32)

    def batch(i, slot):
        s = i // n_tb
        tb = i % n_tb
        for k in range(TB):
            t = tb * TB + k
            for d in range(2):
                d_re = sd_ref[d, 0]
                d_im = sd_ref[d, 1]
                hw_re = hw_ref[t, d, 0]
                hw_im = hw_ref[t, d, 1]
                q_re = d_re * hw_re + d_im * hw_im
                q_im = d_im * hw_re - d_re * hw_im
                col = (2 * k + d) * N2
                q_ref[slot, 0:N1, col:col + N2] = q_re.astype(jnp.bfloat16)
                q_ref[slot, N1:2 * N1, col:col + N2] = q_im.astype(jnp.bfloat16)
        y_ref[slot] = jnp.dot(m1_ref[...], q_ref[slot], preferred_element_type=jnp.float32)
        tc = tc_ref[...]
        ts = ts_ref[...]
        for b in range(nb):
            col = b * N2
            y_re = y_ref[slot, 0:N1, col:col + N2]
            y_im = y_ref[slot, N1:2 * N1, col:col + N2]
            z_re = y_re * tc - y_im * ts
            z_im = y_re * ts + y_im * tc
            z_ref[slot, col:col + N2, 0:N2] = z_re.astype(jnp.bfloat16)
            z_ref[slot, col:col + N2, N2:2 * N2] = z_im.astype(jnp.bfloat16)
        x = jnp.dot(z_ref[slot], m2_ref[...], preferred_element_type=jnp.float32)
        for k in range(TB):
            t = tb * TB + k
            acc = None
            for d in range(2):
                r0 = (2 * k + d) * N1
                x_re = x[r0:r0 + N1, 0:N2]
                x_im = x[r0:r0 + N1, N2:2 * N2]
                p = (x_re * x_re + x_im * x_im) * isig_ref[2 * t + d]
                acc = p if acc is None else acc + p
            best_t = jnp.max(jnp.max(acc, axis=0, keepdims=True), axis=1, keepdims=True)
            lane = lax.broadcasted_iota(jnp.int32, (1, N2), 1)
            row = out_ref[pl.ds(s, 1), :]
            out_ref[pl.ds(s, 1), :] = jnp.where(lane == t, best_t, row)

    def step(j, carry):
        i = 2 * j

        @pl.when(i % n_tb == 0)
        def _():
            seg = i // n_tb
            for d in range(2):
                for part in range(2):
                    sd_ref[d, part] = strain_ref[seg, d, part].astype(jnp.float32)

        batch(i, 0)
        batch(i + 1, 1)
        return carry

    lax.fori_loop(0, out_ref.shape[0] * n_tb // 2, step, 0)


def run_search(isig, strain, tmpl, weights, tables):
    m1, m2, tc, ts = tables
    n_s = strain.shape[0]
    n_t = tmpl.shape[0]
    n_tb = n_t // TB
    vmem = pltpu.VMEM
    smem = pltpu.SMEM
    ffts = n_s * n_t * 2
    cost = pl.CostEstimate(
        flops=ffts * 2 * (2 * 256 * 256 * 128),
        transcendentals=0,
        bytes_accessed=strain.size * 2 + tmpl.size * 2 + weights.size * 4,
    )
    out = pl.pallas_call(
        functools.partial(search_kernel, n_tb),
        out_shape=jax.ShapeDtypeStruct((n_s, N2), jnp.float32),
        in_specs=[pl.BlockSpec(memory_space=smem)] + [pl.BlockSpec(memory_space=vmem)] * 7,
        out_specs=pl.BlockSpec(memory_space=vmem),
        scratch_shapes=[
            pltpu.VMEM((2, 2 * N1, 2 * TB * N2), jnp.bfloat16),
            pltpu.VMEM((2, 2 * N1, 2 * TB * N2), jnp.float32),
            pltpu.VMEM((2, 2 * TB * N1, 2 * N2), jnp.bfloat16),
            pltpu.VMEM((n_t, 2, 2, N1, N2), jnp.float32),
            pltpu.VMEM((2, 2, N1, N2), jnp.float32),
        ],
        cost_estimate=cost,
    )(isig, strain, tmpl, weights, m1, m2, tc, ts)
    return out[:, :n_t]


def swapped(x, axes, size, k):
    return lax.ppermute(x, axes, [(i, i ^ k) for i in range(size)])


def body(strain, templates, psd, flags, assign):
    ya = lax.axis_index("ya")
    n_ya = lax.axis_size("ya")
    n_xh = lax.axis_size("xh")
    n_yb = lax.axis_size("yb")
    n_g = n_xh * n_yb
    g = lax.axis_index("xh") * n_yb + lax.axis_index("yb")

    rows_here = psd.shape[1]
    gathered = jnp.transpose(psd, (1, 0, 2)).reshape(rows_here, -1)
    for axis in ("sc", "z0", "z1", "zh", "sx"):
        gathered = lax.all_gather(gathered, axis, axis=0, tiled=True)
    gathered, strain, templates = lax.optimization_barrier((gathered, strain, templates))
    full_psd = jnp.transpose(gathered.reshape(-1, 2, N2), (1, 0, 2))
    weights = 1.0 / full_psd
    tables = make_tables()

    tmpl_rel = jnp.concatenate(
        [templates] + [swapped(templates, ("xh", "yb"), n_g, k) for k in range(1, n_g)], 0
    )
    pieces = [swapped(strain, "ya", n_ya, k) for k in range(1, n_ya)]
    sigma2 = jax.vmap(lambda tmpl: template_norm(tmpl, weights))(tmpl_rel)
    isig = (1.0 / sigma2).reshape(-1)

    own_count = strain.shape[0]
    first = jnp.concatenate([strain, pieces[0]], 0)
    own_rows = run_search(isig, first, tmpl_rel, weights, tables)
    own_rows, late = lax.optimization_barrier((own_rows, pieces[1:]))
    other_rows = run_search(isig, jnp.concatenate(late, 0), tmpl_rel, weights, tables)
    slots = jnp.concatenate([own_rows, other_rows], 0).reshape(n_ya, own_count, -1)

    lanes = jnp.arange(n_ya, dtype=jnp.int32)
    grouped = jnp.take(slots, ya ^ lanes, axis=0)
    blocks = lax.all_to_all(grouped, "ya", split_axis=0, concat_axis=0, tiled=True)
    blocks = blocks.reshape(n_ya, own_count, n_g, -1)
    src_t = g ^ jnp.arange(n_g, dtype=jnp.int32)
    ordered = jnp.take(blocks, src_t, axis=2)
    ordered = ordered.reshape(n_ya, own_count, n_xh, n_yb, -1)
    rho2 = jnp.transpose(ordered, (1, 2, 0, 3, 4)).reshape(own_count, -1)

    peak = jnp.sqrt(rho2) * flags.astype(jnp.float32)[:, None]
    onehot = assign[:, None] == jnp.arange(BLOCKS, dtype=jnp.int32)[None, :]
    best = jnp.max(jnp.where(onehot[None], peak[:, :, None], jnp.float32(0.0)), axis=1)
    return (peak, best)


def solution(mesh):
    n_seg, n_tpl = mesh.devices.shape
    n_y = 8
    n_xh = n_tpl // n_y
    n_zh = 2
    n_sx = n_seg // (n_zh * 2 * 2 * 2)
    sub = Mesh(
        mesh.devices.reshape(n_sx, n_zh, 2, 2, 2, n_xh, n_y // 2, 2),
        ("sx", "zh", "z1", "z0", "sc", "xh", "ya", "yb"),
    )
    seg = ("sx", "zh", "z1", "z0", "sc")
    rows = seg + ("xh", "ya", "yb")
    placed = (
        P(rows, None, None, None, None),
        P(("xh", "ya", "yb"), None, None, None),
        P(None, seg, None),
        P(rows),
        P(),
    )
    return jax.shard_map(
        body,
        mesh=sub,
        in_specs=placed,
        out_specs=(P(rows, None), P(rows, None)),
        check_vma=False,
    )
```

```python
import functools
import math

import jax
import numpy as np
import jax.numpy as jnp
from jax import lax
from jax.experimental import pallas as pl
from jax.experimental.pallas import tpu as pltpu
from jax.sharding import Mesh
from jax.sharding import PartitionSpec as P

N1 = 128
N2 = 128
BINS = 16384
BLOCKS = 8
TB = 8


def make_tables():
    f32 = np.float32
    row_idx = np.arange(N1, dtype=np.int32)
    col_idx = np.arange(N2, dtype=np.int32)

    def angle(prod, n):
        return (f32(2.0 * math.pi) * (prod % n).astype(f32)) / f32(n)

    ang_one = angle(row_idx[:, None] * row_idx[None, :], N1)
    cos_one = np.cos(ang_one.astype(np.float64)).astype(f32)
    sin_one = np.sin(ang_one.astype(np.float64)).astype(f32)
    first = np.concatenate(
        [np.concatenate([cos_one, -sin_one], 1), np.concatenate([sin_one, cos_one], 1)], 0
    )
    ang_two = angle(col_idx[:, None] * col_idx[None, :], N2)
    cos_two = np.cos(ang_two.astype(np.float64)).astype(f32)
    sin_two = np.sin(ang_two.astype(np.float64)).astype(f32)
    second = np.concatenate(
        [np.concatenate([cos_two, sin_two], 1), np.concatenate([-sin_two, cos_two], 1)], 0
    )
    ang_tw = angle(row_idx[:, None] * col_idx[None, :], BINS)
    tw_cos = np.cos(ang_tw.astype(np.float64)).astype(f32)
    tw_sin = np.sin(ang_tw.astype(np.float64)).astype(f32)
    return (
        jnp.asarray(first, dtype=jnp.bfloat16),
        jnp.asarray(second, dtype=jnp.bfloat16),
        jnp.asarray(tw_cos),
        jnp.asarray(tw_sin),
    )


def template_norm(tmpl, weights):
    h_re = tmpl[0].astype(jnp.float32)
    h_im = tmpl[1].astype(jnp.float32)
    return jnp.sum((h_re * h_re + h_im * h_im) * weights, axis=(1, 2))


def search_kernel(n_tb, n_tp, n_sp, isig_ref, *refs):
    tmpl_refs = refs[:n_tp]
    strain_refs = refs[n_tp:n_tp + n_sp]
    (w_ref, m1_ref, m2_ref, tc_ref, ts_ref, out_ref, q_ref, y_ref, z_ref, hw_ref,
     sd_ref) = refs[n_tp + n_sp:]
    nb = 2 * TB

    per_t = tmpl_refs[0].shape[0]
    for p in range(n_tp):
        def weigh(l, carry, p=p):
            t = p * per_t + l
            h_re = tmpl_refs[p][l, 0].astype(jnp.float32)
            h_im = tmpl_refs[p][l, 1].astype(jnp.float32)
            for d in range(2):
                w = w_ref[d]
                hw_ref[t, d, 0] = h_re * w
                hw_ref[t, d, 1] = h_im * w
            return carry

        lax.fori_loop(0, per_t, weigh, 0)
    out_ref[...] = jnp.zeros(out_ref.shape, jnp.float32)

    def batch(i, slot):
        s = i // n_tb
        tb = i % n_tb
        for k in range(TB):
            t = tb * TB + k
            for d in range(2):
                d_re = sd_ref[d, 0]
                d_im = sd_ref[d, 1]
                hw_re = hw_ref[t, d, 0]
                hw_im = hw_ref[t, d, 1]
                q_re = d_re * hw_re + d_im * hw_im
                q_im = d_im * hw_re - d_re * hw_im
                col = (2 * k + d) * N2
                q_ref[slot, 0:N1, col:col + N2] = q_re.astype(jnp.bfloat16)
                q_ref[slot, N1:2 * N1, col:col + N2] = q_im.astype(jnp.bfloat16)
        y_ref[slot] = jnp.dot(m1_ref[...], q_ref[slot], preferred_element_type=jnp.float32)
        tc = tc_ref[...]
        ts = ts_ref[...]
        for b in range(nb):
            col = b * N2
            y_re = y_ref[slot, 0:N1, col:col + N2]
            y_im = y_ref[slot, N1:2 * N1, col:col + N2]
            z_re = y_re * tc - y_im * ts
            z_im = y_re * ts + y_im * tc
            z_ref[slot, col:col + N2, 0:N2] = z_re.astype(jnp.bfloat16)
            z_ref[slot, col:col + N2, N2:2 * N2] = z_im.astype(jnp.bfloat16)
        x = jnp.dot(z_ref[slot], m2_ref[...], preferred_element_type=jnp.float32)
        for k in range(TB):
            t = tb * TB + k
            acc = None
            for d in range(2):
                r0 = (2 * k + d) * N1
                x_re = x[r0:r0 + N1, 0:N2]
                x_im = x[r0:r0 + N1, N2:2 * N2]
                p = (x_re * x_re + x_im * x_im) * isig_ref[2 * t + d]
                acc = p if acc is None else acc + p
            best_t = jnp.max(jnp.max(acc, axis=0, keepdims=True), axis=1, keepdims=True)
            lane = lax.broadcasted_iota(jnp.int32, (1, N2), 1)
            row = out_ref[pl.ds(s, 1), :]
            out_ref[pl.ds(s, 1), :] = jnp.where(lane == t, best_t, row)

    def step(j, carry):
        i = 2 * j

        @pl.when(i % n_tb == 0)
        def _():
            seg = i // n_tb
            per_s = strain_refs[0].shape[0]
            for p in range(n_sp):
                @pl.when(seg // per_s == p)
                def _(p=p):
                    local = seg - p * per_s
                    for d in range(2):
                        for part in range(2):
                            sd_ref[d, part] = strain_refs[p][local, d, part].astype(jnp.float32)

        batch(i, 0)
        batch(i + 1, 1)
        return carry

    lax.fori_loop(0, out_ref.shape[0] * n_tb // 2, step, 0)


def run_search(isig, strains, tmpls, weights, tables):
    m1, m2, tc, ts = tables
    n_s = sum(x.shape[0] for x in strains)
    n_t = sum(x.shape[0] for x in tmpls)
    n_tb = n_t // TB
    vmem = pltpu.VMEM
    smem = pltpu.SMEM
    ffts = n_s * n_t * 2
    cost = pl.CostEstimate(
        flops=ffts * 2 * (2 * 256 * 256 * 128),
        transcendentals=0,
        bytes_accessed=n_s * strains[0][0].size * 2 + n_t * tmpls[0][0].size * 2 + weights.size * 4,
    )
    out = pl.pallas_call(
        functools.partial(search_kernel, n_tb, len(tmpls), len(strains)),
        out_shape=jax.ShapeDtypeStruct((n_s, N2), jnp.float32),
        in_specs=[pl.BlockSpec(memory_space=smem)]
        + [pl.BlockSpec(memory_space=vmem)] * (len(tmpls) + len(strains) + 5),
        out_specs=pl.BlockSpec(memory_space=vmem),
        scratch_shapes=[
            pltpu.VMEM((2, 2 * N1, 2 * TB * N2), jnp.bfloat16),
            pltpu.VMEM((2, 2 * N1, 2 * TB * N2), jnp.float32),
            pltpu.VMEM((2, 2 * TB * N1, 2 * N2), jnp.bfloat16),
            pltpu.VMEM((n_t, 2, 2, N1, N2), jnp.float32),
            pltpu.VMEM((2, 2, N1, N2), jnp.float32),
        ],
        cost_estimate=cost,
    )(isig, *tmpls, *strains, weights, m1, m2, tc, ts)
    return out[:, :n_t]


def swapped(x, axes, size, k):
    return lax.ppermute(x, axes, [(i, i ^ k) for i in range(size)])


def body(strain, templates, psd, flags, assign):
    ya = lax.axis_index("ya")
    n_ya = lax.axis_size("ya")
    n_xh = lax.axis_size("xh")
    n_yb = lax.axis_size("yb")
    n_g = n_xh * n_yb
    g = lax.axis_index("xh") * n_yb + lax.axis_index("yb")

    rows_here = psd.shape[1]
    gathered = jnp.transpose(psd, (1, 0, 2)).reshape(rows_here, -1)
    for axis in ("sc", "z0", "z1", "zh", "sx"):
        gathered = lax.all_gather(gathered, axis, axis=0, tiled=True)
    gathered, strain, templates = lax.optimization_barrier((gathered, strain, templates))
    full_psd = jnp.transpose(gathered.reshape(-1, 2, N2), (1, 0, 2))
    weights = 1.0 / full_psd
    tables = make_tables()

    tmpl_rel = [templates] + [swapped(templates, ("xh", "yb"), n_g, k) for k in range(1, n_g)]
    pieces = [swapped(strain, "ya", n_ya, k) for k in range(1, n_ya)]
    sigma2 = jnp.concatenate(
        [jax.vmap(lambda tmpl: template_norm(tmpl, weights))(tp) for tp in tmpl_rel], 0
    )
    isig = (1.0 / sigma2).reshape(-1)

    own_count = strain.shape[0]
    own_rows = run_search(isig, [strain], tmpl_rel, weights, tables)
    own_rows, pieces = lax.optimization_barrier((own_rows, pieces))
    other_rows = run_search(isig, pieces, tmpl_rel, weights, tables)
    slots = jnp.concatenate([own_rows, other_rows], 0).reshape(n_ya, own_count, -1)

    lanes = jnp.arange(n_ya, dtype=jnp.int32)
    grouped = jnp.take(slots, ya ^ lanes, axis=0)
    blocks = lax.all_to_all(grouped, "ya", split_axis=0, concat_axis=0, tiled=True)
    blocks = blocks.reshape(n_ya, own_count, n_g, -1)
    src_t = g ^ jnp.arange(n_g, dtype=jnp.int32)
    ordered = jnp.take(blocks, src_t, axis=2)
    ordered = ordered.reshape(n_ya, own_count, n_xh, n_yb, -1)
    rho2 = jnp.transpose(ordered, (1, 2, 0, 3, 4)).reshape(own_count, -1)

    peak = jnp.sqrt(rho2) * flags.astype(jnp.float32)[:, None]
    onehot = assign[:, None] == jnp.arange(BLOCKS, dtype=jnp.int32)[None, :]
    best = jnp.max(jnp.where(onehot[None], peak[:, :, None], jnp.float32(0.0)), axis=1)
    return (peak, best)


def solution(mesh):
    n_seg, n_tpl = mesh.devices.shape
    n_y = 8
    n_xh = n_tpl // n_y
    n_zh = 2
    n_sx = n_seg // (n_zh * 2 * 2 * 2)
    sub = Mesh(
        mesh.devices.reshape(n_sx, n_zh, 2, 2, 2, n_xh, n_y // 2, 2),
        ("sx", "zh", "z1", "z0", "sc", "xh", "ya", "yb"),
    )
    seg = ("sx", "zh", "z1", "z0", "sc")
    rows = seg + ("xh", "ya", "yb")
    placed = (
        P(rows, None, None, None, None),
        P(("xh", "ya", "yb"), None, None, None),
        P(None, seg, None),
        P(rows),
        P(),
    )
    return jax.shard_map(
        body,
        mesh=sub,
        in_specs=placed,
        out_specs=(P(rows, None), P(rows, None)),
        check_vma=False,
    )
```

```python
import functools
import math

import jax
import numpy as np
import jax.numpy as jnp
from jax import lax
from jax.experimental import pallas as pl
from jax.experimental.pallas import tpu as pltpu
from jax.sharding import Mesh
from jax.sharding import PartitionSpec as P

N1 = 128
N2 = 128
BINS = 16384
BLOCKS = 8
TB = 16


def make_tables():
    f32 = np.float32
    row_idx = np.arange(N1, dtype=np.int32)
    col_idx = np.arange(N2, dtype=np.int32)

    def angle(prod, n):
        return (f32(2.0 * math.pi) * (prod % n).astype(f32)) / f32(n)

    ang_one = angle(row_idx[:, None] * row_idx[None, :], N1)
    cos_one = np.cos(ang_one.astype(np.float64)).astype(f32)
    sin_one = np.sin(ang_one.astype(np.float64)).astype(f32)
    first = np.concatenate(
        [np.concatenate([cos_one, -sin_one], 1), np.concatenate([sin_one, cos_one], 1)], 0
    )
    ang_two = angle(col_idx[:, None] * col_idx[None, :], N2)
    cos_two = np.cos(ang_two.astype(np.float64)).astype(f32)
    sin_two = np.sin(ang_two.astype(np.float64)).astype(f32)
    second = np.concatenate(
        [np.concatenate([cos_two, sin_two], 1), np.concatenate([-sin_two, cos_two], 1)], 0
    )
    ang_tw = angle(row_idx[:, None] * col_idx[None, :], BINS)
    tw_cos = np.cos(ang_tw.astype(np.float64)).astype(f32)
    tw_sin = np.sin(ang_tw.astype(np.float64)).astype(f32)
    return (
        jnp.asarray(first, dtype=jnp.bfloat16),
        jnp.asarray(second, dtype=jnp.bfloat16),
        jnp.asarray(tw_cos),
        jnp.asarray(tw_sin),
    )


def template_norm(tmpl, weights):
    h_re = tmpl[0].astype(jnp.float32)
    h_im = tmpl[1].astype(jnp.float32)
    return jnp.sum((h_re * h_re + h_im * h_im) * weights, axis=(1, 2))


def search_kernel(n_tb, isig_ref, strain_ref, tmpl_ref, w_ref, m1_ref, m2_ref,
                  tc_ref, ts_ref, out_ref, q_ref, y_ref, z_ref, hw_ref, sd_ref):
    nb = 2 * TB

    def weigh(t, carry):
        h_re = tmpl_ref[t, 0].astype(jnp.float32)
        h_im = tmpl_ref[t, 1].astype(jnp.float32)
        for d in range(2):
            w = w_ref[d]
            hw_ref[t, d, 0] = h_re * w
            hw_ref[t, d, 1] = h_im * w
        return carry

    lax.fori_loop(0, tmpl_ref.shape[0], weigh, 0)
    out_ref[...] = jnp.zeros(out_ref.shape, jnp.float32)

    def batch(i, slot, src):
        s = i // n_tb
        tb = i % n_tb
        for k in range(TB):
            t = tb * TB + k
            for d in range(2):
                d_re = sd_ref[src, d, 0]
                d_im = sd_ref[src, d, 1]
                hw_re = hw_ref[t, d, 0]
                hw_im = hw_ref[t, d, 1]
                q_re = d_re * hw_re + d_im * hw_im
                q_im = d_im * hw_re - d_re * hw_im
                col = (2 * k + d) * N2
                q_ref[slot, 0:N1, col:col + N2] = q_re.astype(jnp.bfloat16)
                q_ref[slot, N1:2 * N1, col:col + N2] = q_im.astype(jnp.bfloat16)
        y_ref[slot] = jnp.dot(m1_ref[...], q_ref[slot], preferred_element_type=jnp.float32)
        tc = tc_ref[...]
        ts = ts_ref[...]
        for b in range(nb):
            col = b * N2
            y_re = y_ref[slot, 0:N1, col:col + N2]
            y_im = y_ref[slot, N1:2 * N1, col:col + N2]
            z_re = y_re * tc - y_im * ts
            z_im = y_re * ts + y_im * tc
            z_ref[slot, col:col + N2, 0:N2] = z_re.astype(jnp.bfloat16)
            z_ref[slot, col:col + N2, N2:2 * N2] = z_im.astype(jnp.bfloat16)
        x = jnp.dot(z_ref[slot], m2_ref[...], preferred_element_type=jnp.float32)
        for k in range(TB):
            t = tb * TB + k
            acc = None
            for d in range(2):
                r0 = (2 * k + d) * N1
                x_re = x[r0:r0 + N1, 0:N2]
                x_im = x[r0:r0 + N1, N2:2 * N2]
                p = (x_re * x_re + x_im * x_im) * isig_ref[2 * t + d]
                acc = p if acc is None else acc + p
            best_t = jnp.max(jnp.max(acc, axis=0, keepdims=True), axis=1, keepdims=True)
            lane = lax.broadcasted_iota(jnp.int32, (1, N2), 1)
            row = out_ref[pl.ds(s, 1), :]
            out_ref[pl.ds(s, 1), :] = jnp.where(lane == t, best_t, row)

    def step(j, carry):
        i = 2 * j

        if n_tb == 1:
            for slot in range(2):
                for d in range(2):
                    for part in range(2):
                        sd_ref[slot, d, part] = strain_ref[i + slot, d, part].astype(jnp.float32)
            batch(i, 0, 0)
            batch(i + 1, 1, 1)
        else:
            @pl.when(i % n_tb == 0)
            def _():
                seg = i // n_tb
                for d in range(2):
                    for part in range(2):
                        sd_ref[0, d, part] = strain_ref[seg, d, part].astype(jnp.float32)

            batch(i, 0, 0)
            batch(i + 1, 1, 0)
        return carry

    lax.fori_loop(0, out_ref.shape[0] * n_tb // 2, step, 0)


def run_search(isig, strain, tmpl, weights, tables):
    m1, m2, tc, ts = tables
    n_s = strain.shape[0]
    n_t = tmpl.shape[0]
    n_tb = n_t // TB
    vmem = pltpu.VMEM
    smem = pltpu.SMEM
    ffts = n_s * n_t * 2
    cost = pl.CostEstimate(
        flops=ffts * 2 * (2 * 256 * 256 * 128),
        transcendentals=0,
        bytes_accessed=strain.size * 2 + tmpl.size * 2 + weights.size * 4,
    )
    out = pl.pallas_call(
        functools.partial(search_kernel, n_tb),
        out_shape=jax.ShapeDtypeStruct((n_s, N2), jnp.float32),
        in_specs=[pl.BlockSpec(memory_space=smem)] + [pl.BlockSpec(memory_space=vmem)] * 7,
        out_specs=pl.BlockSpec(memory_space=vmem),
        scratch_shapes=[
            pltpu.VMEM((2, 2 * N1, 2 * TB * N2), jnp.bfloat16),
            pltpu.VMEM((2, 2 * N1, 2 * TB * N2), jnp.float32),
            pltpu.VMEM((2, 2 * TB * N1, 2 * N2), jnp.bfloat16),
            pltpu.VMEM((n_t, 2, 2, N1, N2), jnp.float32),
            pltpu.VMEM((2, 2, 2, N1, N2), jnp.float32),
        ],
        cost_estimate=cost,
    )(isig, strain, tmpl, weights, m1, m2, tc, ts)
    return out[:, :n_t]


def swapped(x, axes, size, k):
    return lax.ppermute(x, axes, [(i, i ^ k) for i in range(size)])


def body(strain, templates, psd, flags, assign):
    ya = lax.axis_index("ya")
    n_ya = lax.axis_size("ya")
    n_xh = lax.axis_size("xh")
    n_yb = lax.axis_size("yb")
    n_g = n_xh * n_yb
    g = lax.axis_index("xh") * n_yb + lax.axis_index("yb")

    rows_here = psd.shape[1]
    gathered = jnp.transpose(psd, (1, 0, 2)).reshape(rows_here, -1)
    for axis in ("sc", "z0", "z1", "zh", "sx"):
        gathered = lax.all_gather(gathered, axis, axis=0, tiled=True)
    gathered, strain, templates = lax.optimization_barrier((gathered, strain, templates))
    full_psd = jnp.transpose(gathered.reshape(-1, 2, N2), (1, 0, 2))
    weights = 1.0 / full_psd
    tables = make_tables()

    tmpl_rel = jnp.concatenate(
        [templates] + [swapped(templates, ("xh", "yb"), n_g, k) for k in range(1, n_g)], 0
    )
    piece = jnp.concatenate([swapped(strain, "ya", n_ya, k) for k in range(1, n_ya)], 0)
    sigma2 = jax.vmap(lambda tmpl: template_norm(tmpl, weights))(tmpl_rel)
    isig = (1.0 / sigma2).reshape(-1)

    own_count = strain.shape[0]
    own_rows = run_search(isig, strain, tmpl_rel, weights, tables)
    own_rows, piece = lax.optimization_barrier((own_rows, piece))
    other_rows = run_search(isig, piece, tmpl_rel, weights, tables)
    slots = jnp.concatenate([own_rows, other_rows], 0).reshape(n_ya, own_count, -1)

    lanes = jnp.arange(n_ya, dtype=jnp.int32)
    grouped = jnp.take(slots, ya ^ lanes, axis=0)
    blocks = lax.all_to_all(grouped, "ya", split_axis=0, concat_axis=0, tiled=True)
    blocks = blocks.reshape(n_ya, own_count, n_g, -1)
    src_t = g ^ jnp.arange(n_g, dtype=jnp.int32)
    ordered = jnp.take(blocks, src_t, axis=2)
    ordered = ordered.reshape(n_ya, own_count, n_xh, n_yb, -1)
    rho2 = jnp.transpose(ordered, (1, 2, 0, 3, 4)).reshape(own_count, -1)

    peak = jnp.sqrt(rho2) * flags.astype(jnp.float32)[:, None]
    onehot = assign[:, None] == jnp.arange(BLOCKS, dtype=jnp.int32)[None, :]
    best = jnp.max(jnp.where(onehot[None], peak[:, :, None], jnp.float32(0.0)), axis=1)
    return (peak, best)


def solution(mesh):
    n_seg, n_tpl = mesh.devices.shape
    n_y = 8
    n_xh = n_tpl // n_y
    n_zh = 2
    n_sx = n_seg // (n_zh * 2 * 2 * 2)
    sub = Mesh(
        mesh.devices.reshape(n_sx, n_zh, 2, 2, 2, n_xh, n_y // 2, 2),
        ("sx", "zh", "z1", "z0", "sc", "xh", "ya", "yb"),
    )
    seg = ("sx", "zh", "z1", "z0", "sc")
    rows = seg + ("xh", "ya", "yb")
    placed = (
        P(rows, None, None, None, None),
        P(("xh", "ya", "yb"), None, None, None),
        P(None, seg, None),
        P(rows),
        P(),
    )
    return jax.shard_map(
        body,
        mesh=sub,
        in_specs=placed,
        out_specs=(P(rows, None), P(rows, None)),
        check_vma=False,
    )
```
